32 devices in a mesh: mesh: 8 (over z, x), view: 4 (over y, core).
Axes of the slice: x: 2, y: 2, z: 4, core: 2. Of those that a mesh axis runs over, the one named last changes fastest.
Arguments:
- queries: bfloat16 [6144, 1280], P(('mesh', 'view')), may hold values from -6 to 6
- keys: bfloat16 [6144, 1280], P(('mesh', 'view')), may hold values from -6 to 6
- values: bfloat16 [6144, 1280], P(('mesh', 'view')), may hold values from -6 to 6
- ref_keys: bfloat16 [1024, 1280], P(('mesh', 'view')), may hold values from -6 to 6
- ref_values: bfloat16 [1024, 1280], P(('mesh', 'view')), may hold values from -6 to 6
- out_weight: bfloat16 [1280, 1280], replicated, may hold values from -0.15625 to 0.15625
- adjacency: int32 [48, 3], P('mesh'), may hold values from 0 to 5, as said below
- ref_source: int32 [1], replicated, may hold values from 0 to 7
Outputs:
- blended: bfloat16 [6144, 1280], P(('mesh', 'view'))
The draws below stay inside these ranges and needn't reach their ends.
Inputs may be any that keep to these rules, and one draw needn't show every extreme that they name: `adjacency`: each row lists 3 different views of the same mesh, never the row's own view.
All inputs are finite; a program needn't handle non-finite values.
Results may differ from the reference program's by a relative error of at most 0.0055.
Values may be sent and summed in bfloat16 or wider, within the bound.
No kernel may reach another device: no remote copies, remote signals or barrier semaphores. Data moves between devices by JAX's collectives and lax.ppermute only.
A program may use at most 128 MiB of HBM per device.

```python
import jax
import jax.numpy as jnp
from jax import lax

HEADS = 20
HEAD_DIM = 64
D = 1280
VIEWS = 6
VIEW_TOK = 128
ADJ = 3
MESHES = 8
REF_TOK = 128


def draw_base(key, rows):
    return jnp.clip(1.5 * jax.random.normal(key, (rows, D), jnp.float32), -6.0, 6.0)


def drawn_keys(key, salt, rows):
    drawn = draw_base(jax.random.fold_in(key, salt), rows)
    return drawn.astype(jnp.bfloat16)


def draw_queries(key, part):
    rows = MESHES * VIEWS * VIEW_TOK
    drawn = draw_base(jax.random.fold_in(key, 11), rows)
    return drawn.astype(jnp.bfloat16)


def draw_keys(key, part):
    return drawn_keys(key, 12, MESHES * VIEWS * VIEW_TOK)


def draw_ref_keys(key, part):
    return drawn_keys(key, 13, MESHES * REF_TOK)


def draw_adjacency(key, part):
    scores = jax.random.randint(jax.random.fold_in(key, 21), (MESHES, VIEWS, VIEWS), 0, 1 << 20)
    distinct = scores * VIEWS + jnp.arange(VIEWS, dtype=jnp.int32)[None, None, :]
    itself = jnp.arange(VIEWS, dtype=jnp.int32)[:, None] == jnp.arange(VIEWS, dtype=jnp.int32)[None, :]
    distinct = jnp.where(itself[None, :, :], -1, distinct)
    unused, picked = lax.top_k(distinct, ADJ)
    return picked.astype(jnp.int32).reshape(MESHES * VIEWS, ADJ)


def block_scale(own_key, shape, shards, low, high):
    level, own = 1.0, jax.random.fold_in(own_key, 6)
    for position, blocks in shards:
        draws = jnp.exp(jax.random.uniform(jax.random.fold_in(own, position), (blocks,), jnp.float32, low / len(shards), high / len(shards)))
        level = level * jnp.repeat(draws, shape[position] // blocks).reshape([-1 if axis == position else 1 for axis in range(len(shape))])
    return level


def bell_draw(own_key, extent, spread, bound, shards=(), held_as=jnp.bfloat16):
    values = jax.random.normal(own_key, extent, jnp.float32) * spread
    if len(shards) > 0:
        values = block_scale(own_key, extent, shards, -0.22, 0.18) * values
    return jnp.clip(values, min=-bound, max=bound).astype(held_as)


def setup_inputs(seed: int = 0) -> dict:
    splits = jax.random.split(jax.random.key(seed), 9)
    return {
        "queries": draw_queries(jax.random.fold_in(splits[8], 71), 0),
        "keys": draw_keys(jax.random.fold_in(splits[8], 71), 0),
        "values": bell_draw(splits[2], (MESHES * VIEWS * VIEW_TOK, D), 1.0, 6.0, ((0, 32),)),
        "ref_keys": draw_ref_keys(jax.random.fold_in(splits[8], 71), 0),
        "ref_values": bell_draw(splits[4], (MESHES * REF_TOK, D), 1.0, 6.0, ((0, 32),)),
        "out_weight": bell_draw(splits[5], (D, D), D ** -0.5, 0.15625),
        "adjacency": draw_adjacency(jax.random.fold_in(splits[8], 71), 0),
        "ref_source": jax.random.randint(splits[7], (1,), 0, MESHES).astype(jnp.int32),
    }


SCALE = 0.125


def attend(query_rows, key_rows, value_rows):
    scores = jnp.einsum("qhd,khd->hqk", query_rows.astype(jnp.float32), key_rows.astype(jnp.float32)) * SCALE
    peak = jnp.max(scores, axis=-1, keepdims=True)
    weights = jnp.exp(scores - peak)
    totals = jnp.sum(weights, axis=-1)
    rounded = weights.astype(jnp.bfloat16)
    summed = jnp.einsum("hqk,khd->qhd", rounded.astype(jnp.float32), value_rows.astype(jnp.float32))
    return summed / jnp.transpose(totals)[:, :, None]


def reference(queries, keys, values, ref_keys, ref_values, out_weight, adjacency, ref_source):
    query_grid = queries.reshape(MESHES, VIEWS, VIEW_TOK, HEADS, HEAD_DIM)
    key_grid = keys.reshape(MESHES, VIEWS, VIEW_TOK, HEADS, HEAD_DIM)
    value_grid = values.reshape(MESHES, VIEWS, VIEW_TOK, HEADS, HEAD_DIM)
    ref_key_grid = ref_keys.reshape(MESHES, REF_TOK, HEADS, HEAD_DIM)
    ref_value_grid = ref_values.reshape(MESHES, REF_TOK, HEADS, HEAD_DIM)
    source = ref_source[0]
    shared_keys = ref_key_grid[source]
    shared_values = ref_value_grid[source]
    adjacent = adjacency.reshape(MESHES, VIEWS, ADJ)

    def one_view(flat_index):
        mesh_index = flat_index // VIEWS
        view_index = flat_index % VIEWS
        own_queries = query_grid[mesh_index, view_index]
        chosen = jnp.concatenate([view_index.reshape(1).astype(jnp.int32), adjacent[mesh_index, view_index].astype(jnp.int32)])
        picked_keys = key_grid[mesh_index][chosen].reshape((ADJ + 1) * VIEW_TOK, HEADS, HEAD_DIM)
        picked_values = value_grid[mesh_index][chosen].reshape((ADJ + 1) * VIEW_TOK, HEADS, HEAD_DIM)
        view_part = attend(own_queries, picked_keys, picked_values)
        ref_part = attend(own_queries, shared_keys, shared_values)
        mixed = (view_part + ref_part).reshape(VIEW_TOK, HEADS * HEAD_DIM).astype(jnp.bfloat16)
        return jnp.dot(mixed, out_weight, preferred_element_type=jnp.float32).astype(jnp.bfloat16)

    outputs = lax.map(one_view, jnp.arange(MESHES * VIEWS, dtype=jnp.int32))
    return outputs.reshape(MESHES * VIEWS * VIEW_TOK, HEADS * HEAD_DIM)
```

```python
import functools

import jax
import jax.numpy as jnp
from jax import lax
from jax.experimental import pallas as pl
from jax.experimental.pallas import tpu as pltpu
from jax.sharding import PartitionSpec as P

HEADS = 20
HEAD_DIM = 64
VIEWS = 6
ADJ = 3
SCALE = 0.125
LANES = 128


def tree_broadcast(value, axis, source):
    count = lax.axis_size(axis)
    index = lax.axis_index(axis)
    if count & (count - 1):
        kept = jnp.where(index == source, value, jnp.zeros_like(value))
        return lax.psum(kept, axis)
    distance = 1
    while distance < count:
        pairs = [(i, i ^ distance) for i in range(count)]
        received = lax.ppermute(value, axis, pairs)
        partner_has = ((index ^ distance) // distance) == (source // distance)
        value = jnp.where(partner_has, received, value)
        distance *= 2
    return value


def gather_pieces(value, axis):
    count = lax.axis_size(axis)
    index = lax.axis_index(axis)
    if count == 4:
        across = lax.ppermute(value, axis, [(i, i ^ 2) for i in range(count)])
        both = jnp.concatenate([value, across], axis=0)
        near = lax.ppermute(both, axis, [(i, i ^ 1) for i in range(count)])
        positions = jnp.stack([index, index ^ 2, index ^ 1, index ^ 3])
        return [both, near], positions
    whole = lax.all_gather(value, axis, axis=0, tiled=True)
    return [whole], jnp.arange(count, dtype=jnp.int32)


def attention_kernel(piece_count, q_ref, *refs):
    key_refs = refs[: 2 * piece_count]
    rk_ref, rv_ref, bias_ref, out_ref = refs[2 * piece_count :]
    queries = q_ref[...]
    lane = lax.broadcasted_iota(jnp.int32, (1, LANES), 1)
    bias = bias_ref[...]
    dims = (((1,), (1,)), ((), ()))
    results = []
    for head in range(LANES // HEAD_DIM):
        own = (lane // HEAD_DIM) == head
        q_head = jnp.where(own, queries, jnp.zeros_like(queries))
        scores = [
            lax.dot_general(q_head, key_refs[2 * p][...], dims, preferred_element_type=jnp.float32)
            for p in range(piece_count)
        ]
        scores = jnp.concatenate(scores, axis=1) * SCALE + bias
        peak = jnp.max(scores, axis=1, keepdims=True)
        weights = jnp.exp(scores - peak)
        total = jnp.sum(weights, axis=1, keepdims=True)
        rounded = weights.astype(jnp.bfloat16)
        summed = None
        start = 0
        for p in range(piece_count):
            values = key_refs[2 * p + 1][...]
            rows = values.shape[0]
            part = jnp.dot(rounded[:, start : start + rows], values, preferred_element_type=jnp.float32)
            summed = part if summed is None else summed + part
            start += rows
        view_part = summed / total
        ref_scores = (
            lax.dot_general(q_head, rk_ref[...], dims, preferred_element_type=jnp.float32) * SCALE
        )
        ref_peak = jnp.max(ref_scores, axis=1, keepdims=True)
        ref_weights = jnp.exp(ref_scores - ref_peak)
        ref_total = jnp.sum(ref_weights, axis=1, keepdims=True)
        ref_summed = jnp.dot(
            ref_weights.astype(jnp.bfloat16), rv_ref[...], preferred_element_type=jnp.float32
        )
        results.append((own, view_part + ref_summed / ref_total))
    mixed = results[-1][1]
    for own, value in results[:-1]:
        mixed = jnp.where(own, value, mixed)
    out_ref[...] = mixed.astype(out_ref.dtype)


def attention(queries, pieces, ref_both, bias, width):
    rows = queries.shape[0]
    blocks = width // LANES
    in_specs = [pl.BlockSpec((rows, LANES), lambda j: (0, j))]
    operands = [queries]
    for piece in pieces:
        in_specs.append(pl.BlockSpec((piece.shape[0], LANES), lambda j: (0, j)))
        in_specs.append(pl.BlockSpec((piece.shape[0], LANES), lambda j: (0, j + blocks)))
        operands += [piece, piece]
    ref_rows = ref_both.shape[0]
    in_specs.append(pl.BlockSpec((ref_rows, LANES), lambda j: (0, j)))
    in_specs.append(pl.BlockSpec((ref_rows, LANES), lambda j: (0, j + blocks)))
    operands += [ref_both, ref_both]
    in_specs.append(pl.BlockSpec(bias.shape, lambda j: (0, 0)))
    operands.append(bias)
    keys = sum(piece.shape[0] for piece in pieces)
    flops = 4 * rows * (keys + ref_rows) * width * 2
    return pl.pallas_call(
        functools.partial(attention_kernel, len(pieces)),
        grid=(blocks,),
        in_specs=in_specs,
        out_specs=pl.BlockSpec((rows, LANES), lambda j: (0, j)),
        out_shape=jax.ShapeDtypeStruct((rows, width), jnp.bfloat16),
        compiler_params=pltpu.CompilerParams(
            dimension_semantics=("arbitrary",), vmem_limit_bytes=48 * 1024 * 1024
        ),
        cost_estimate=pl.CostEstimate(
            flops=flops,
            transcendentals=2 * rows * (keys + ref_rows) * HEADS,
            bytes_accessed=2 * (rows * width * 2 + (keys + ref_rows) * width * 2) + 4 * rows * keys,
        ),
    )(*operands)


def body(queries, keys, values, ref_keys, ref_values, out_weight, adjacency, ref_source):
    shard_rows, width = queries.shape
    view_count = lax.axis_size("view")
    view_index = lax.axis_index("view")
    view_tok = shard_rows * view_count // VIEWS

    ref_both = jnp.concatenate([ref_keys, ref_values], axis=1)
    ref_shared = tree_broadcast(ref_both, "mesh", ref_source[0])
    ref_pieces, unused = gather_pieces(ref_shared, "view")
    ref_all = ref_pieces[0] if len(ref_pieces) == 1 else jnp.concatenate(ref_pieces, axis=0)

    both = jnp.concatenate([keys, values], axis=1)
    pieces, positions = gather_pieces(both, "view")

    view_ids = jnp.arange(VIEWS, dtype=jnp.int32)
    listed = jnp.any(adjacency[:, :, None] == view_ids[None, None, :], axis=1)
    allowed = listed | (view_ids[:, None] == view_ids[None, :])
    query_views = (view_index * shard_rows + jnp.arange(shard_rows, dtype=jnp.int32)) // view_tok
    key_rows = (positions[:, None] * shard_rows + jnp.arange(shard_rows, dtype=jnp.int32)[None, :]).reshape(-1)
    key_views = key_rows // view_tok
    keep = allowed[query_views[:, None], key_views[None, :]]
    bias = jnp.where(keep, 0.0, -jnp.inf).astype(jnp.float32)

    mixed = attention(queries, pieces, ref_all, bias, width)
    return jnp.dot(mixed, out_weight, preferred_element_type=jnp.float32).astype(jnp.bfloat16)


def solution(mesh):
    return jax.shard_map(
        body,
        mesh=mesh,
        in_specs=(
            P(("mesh", "view"), None),
            P(("mesh", "view"), None),
            P(("mesh", "view"), None),
            P(("mesh", "view"), None),
            P(("mesh", "view"), None),
            P(),
            P("mesh", None),
            P(),
        ),
        out_specs=P(("mesh", "view"), None),
        check_vma=False,
    )
```

```python
import functools

import jax
import jax.numpy as jnp
from jax import lax
from jax.experimental import pallas as pl
from jax.experimental.pallas import tpu as pltpu
from jax.sharding import PartitionSpec as P

HEADS = 20
HEAD_DIM = 64
VIEWS = 6
ADJ = 3
SCALE = 0.125
LANES = 128


def tree_broadcast(value, axis, source):
    count = lax.axis_size(axis)
    index = lax.axis_index(axis)
    if count & (count - 1):
        kept = jnp.where(index == source, value, jnp.zeros_like(value))
        return lax.psum(kept, axis)
    distance = 1
    while distance < count:
        pairs = [(i, i ^ distance) for i in range(count)]
        received = lax.ppermute(value, axis, pairs)
        partner_has = ((index ^ distance) // distance) == (source // distance)
        value = jnp.where(partner_has, received, value)
        distance *= 2
    return value


def gather_pieces(value, axis):
    count = lax.axis_size(axis)
    index = lax.axis_index(axis)
    if count == 4:
        across = lax.ppermute(value, axis, [(i, i ^ 2) for i in range(count)])
        both = jnp.concatenate([value, across], axis=0)
        near = lax.ppermute(both, axis, [(i, i ^ 1) for i in range(count)])
        positions = jnp.stack([index, index ^ 2, index ^ 1, index ^ 3])
        return [both, near], positions
    whole = lax.all_gather(value, axis, axis=0, tiled=True)
    return [whole], jnp.arange(count, dtype=jnp.int32)


def attention_kernel(piece_count, q_ref, *refs):
    key_refs = refs[: 2 * piece_count]
    rk_ref, rv_ref, bias_ref, out_ref = refs[2 * piece_count :]
    queries = q_ref[...]
    lane = lax.broadcasted_iota(jnp.int32, (1, LANES), 1)
    bias = bias_ref[...]
    dims = (((1,), (1,)), ((), ()))
    results = []
    for head in range(LANES // HEAD_DIM):
        own = (lane // HEAD_DIM) == head
        q_head = jnp.where(own, queries, jnp.zeros_like(queries))
        scores = [
            lax.dot_general(q_head, key_refs[2 * p][...], dims, preferred_element_type=jnp.float32)
            for p in range(piece_count)
        ]
        scores = jnp.concatenate(scores, axis=1) * SCALE + bias
        peak = jnp.max(scores, axis=1, keepdims=True)
        weights = jnp.exp(scores - peak)
        total = jnp.sum(weights, axis=1, keepdims=True)
        rounded = weights.astype(jnp.bfloat16)
        summed = None
        start = 0
        for p in range(piece_count):
            values = key_refs[2 * p + 1][...]
            rows = values.shape[0]
            part = jnp.dot(rounded[:, start : start + rows], values, preferred_element_type=jnp.float32)
            summed = part if summed is None else summed + part
            start += rows
        view_part = summed / total
        ref_scores = (
            lax.dot_general(q_head, rk_ref[...], dims, preferred_element_type=jnp.float32) * SCALE
        )
        ref_peak = jnp.max(ref_scores, axis=1, keepdims=True)
        ref_weights = jnp.exp(ref_scores - ref_peak)
        ref_total = jnp.sum(ref_weights, axis=1, keepdims=True)
        ref_summed = jnp.dot(
            ref_weights.astype(jnp.bfloat16), rv_ref[...], preferred_element_type=jnp.float32
        )
        results.append((own, view_part + ref_summed / ref_total))
    mixed = results[-1][1]
    for own, value in results[:-1]:
        mixed = jnp.where(own, value, mixed)
    out_ref[...] = mixed.astype(out_ref.dtype)


def attention(queries, pieces, ref_both, bias, width):
    rows = queries.shape[0]
    blocks = width // LANES
    in_specs = [pl.BlockSpec((rows, LANES), lambda j: (0, j))]
    operands = [queries]
    for piece in pieces:
        in_specs.append(pl.BlockSpec((piece.shape[0], LANES), lambda j: (0, j)))
        in_specs.append(pl.BlockSpec((piece.shape[0], LANES), lambda j: (0, j + blocks)))
        operands += [piece, piece]
    ref_rows = ref_both.shape[0]
    in_specs.append(pl.BlockSpec((ref_rows, LANES), lambda j: (0, j)))
    in_specs.append(pl.BlockSpec((ref_rows, LANES), lambda j: (0, j + blocks)))
    operands += [ref_both, ref_both]
    in_specs.append(pl.BlockSpec(bias.shape, lambda j: (0, 0)))
    operands.append(bias)
    keys = sum(piece.shape[0] for piece in pieces)
    flops = 4 * rows * (keys + ref_rows) * width * 2
    return pl.pallas_call(
        functools.partial(attention_kernel, len(pieces)),
        grid=(blocks,),
        in_specs=in_specs,
        out_specs=pl.BlockSpec((rows, LANES), lambda j: (0, j)),
        out_shape=jax.ShapeDtypeStruct((rows, width), jnp.bfloat16),
        compiler_params=pltpu.CompilerParams(
            dimension_semantics=("arbitrary",), vmem_limit_bytes=48 * 1024 * 1024
        ),
        cost_estimate=pl.CostEstimate(
            flops=flops,
            transcendentals=2 * rows * (keys + ref_rows) * HEADS,
            bytes_accessed=2 * (rows * width * 2 + (keys + ref_rows) * width * 2) + 4 * rows * keys,
        ),
    )(*operands)


def body(queries, keys, values, ref_keys, ref_values, out_weight, adjacency, ref_source):
    shard_rows, width = queries.shape
    view_count = lax.axis_size("view")
    view_index = lax.axis_index("view")
    view_tok = shard_rows * view_count // VIEWS

    ref_both = jnp.concatenate([ref_keys, ref_values], axis=1)
    ref_shared = tree_broadcast(ref_both, "mesh", ref_source[0])
    ref_pieces, unused = gather_pieces(ref_shared, "view")
    ref_all = ref_pieces[0] if len(ref_pieces) == 1 else jnp.concatenate(ref_pieces, axis=0)

    both = jnp.concatenate([keys, values], axis=1)
    pieces, positions = gather_pieces(both, "view")

    view_ids = jnp.arange(VIEWS, dtype=jnp.int32)
    query_views = (view_index * shard_rows + jnp.arange(shard_rows, dtype=jnp.int32)) // view_tok
    key_rows = (positions[:, None] * shard_rows + jnp.arange(shard_rows, dtype=jnp.int32)[None, :]).reshape(-1)
    key_views = key_rows // view_tok
    query_onehot = (query_views[:, None] == view_ids[None, :]).astype(jnp.float32)
    query_adjacent = jnp.dot(query_onehot, adjacency.astype(jnp.float32))
    keep = query_views[:, None] == key_views[None, :]
    for slot in range(ADJ):
        keep = keep | (query_adjacent[:, slot : slot + 1] == key_views[None, :].astype(jnp.float32))
    bias = jnp.where(keep, 0.0, -jnp.inf).astype(jnp.float32)

    mixed = attention(queries, pieces, ref_all, bias, width)
    return jnp.dot(mixed, out_weight, preferred_element_type=jnp.float32).astype(jnp.bfloat16)


def solution(mesh):
    return jax.shard_map(
        body,
        mesh=mesh,
        in_specs=(
            P(("mesh", "view"), None),
            P(("mesh", "view"), None),
            P(("mesh", "view"), None),
            P(("mesh", "view"), None),
            P(("mesh", "view"), None),
            P(),
            P("mesh", None),
            P(),
        ),
        out_specs=P(("mesh", "view"), None),
        check_vma=False,
    )
```

```python
import functools

import jax
import jax.numpy as jnp
from jax import lax
from jax.experimental import pallas as pl
from jax.experimental.pallas import tpu as pltpu
from jax.sharding import PartitionSpec as P

HEADS = 20
HEAD_DIM = 64
VIEWS = 6
ADJ = 3
SCALE = 0.125
LANES = 128


def tree_broadcast(value, axis, source):
    count = lax.axis_size(axis)
    index = lax.axis_index(axis)
    if count & (count - 1):
        kept = jax.tree.map(lambda a: jnp.where(index == source, a, jnp.zeros_like(a)), value)
        return lax.psum(kept, axis)
    distance = 1
    while distance < count:
        pairs = [(i, i ^ distance) for i in range(count)]
        received = lax.ppermute(value, axis, pairs)
        partner_has = ((index ^ distance) // distance) == (source // distance)
        value = jax.tree.map(lambda r, a: jnp.where(partner_has, r, a), received, value)
        distance *= 2
    return value


def gather_rows(value, axis):
    count = lax.axis_size(axis)
    if count == 4:
        across = lax.ppermute(value, axis, [(i, i ^ 2) for i in range(count)])
        both = jax.tree.map(lambda a, b: jnp.concatenate([a, b], axis=0), value, across)
        near = lax.ppermute(both, axis, [(i, i ^ 1) for i in range(count)])
        return jax.tree.map(lambda a, b: jnp.concatenate([a, b], axis=0), both, near)
    return lax.all_gather(value, axis, axis=0, tiled=True)


def absorb_kernel(first, final, q_ref, k_ref, v_ref, bias_ref, *rest):
    rest = list(rest)
    if not first:
        m_in, t_in, acc_in = rest[:3]
        rest = rest[3:]
    if final:
        rk_ref, rv_ref, out_ref = rest
    else:
        m_out, t_out, acc_out = rest
    step = pl.program_id(0)
    rows = q_ref.shape[0]
    queries = q_ref[...]
    lane = lax.broadcasted_iota(jnp.int32, (1, LANES), 1)
    bias = bias_ref[...]
    dims = (((1,), (1,)), ((), ()))
    if first:
        m_cur = jnp.full((rows, LANES), -1e30, jnp.float32)
        t_cur = jnp.zeros((rows, LANES), jnp.float32)
        acc_old = jnp.zeros((rows, LANES), jnp.float32)
    else:
        m_cur = m_in[...]
        t_cur = t_in[...]
        acc_old = acc_in[...]
    keys = k_ref[...]
    values = v_ref[...]
    results = []
    for head in range(LANES // HEAD_DIM):
        own = (lane // HEAD_DIM) == head
        picked = lane == step * (LANES // HEAD_DIM) + head
        m_old = jnp.sum(jnp.where(picked, m_cur, 0.0), axis=1, keepdims=True)
        t_old = jnp.sum(jnp.where(picked, t_cur, 0.0), axis=1, keepdims=True)
        q_head = jnp.where(own, queries, jnp.zeros_like(queries))
        scores = lax.dot_general(q_head, keys, dims, preferred_element_type=jnp.float32) * SCALE + bias
        m_new = jnp.maximum(m_old, jnp.max(scores, axis=1, keepdims=True))
        alpha = jnp.exp(m_old - m_new)
        weights = jnp.exp(scores - m_new)
        t_new = alpha * t_old + jnp.sum(weights, axis=1, keepdims=True)
        summed = alpha * acc_old + jnp.dot(
            weights.astype(jnp.bfloat16), values, preferred_element_type=jnp.float32
        )
        if final:
            ref_scores = (
                lax.dot_general(q_head, rk_ref[...], dims, preferred_element_type=jnp.float32) * SCALE
            )
            ref_peak = jnp.max(ref_scores, axis=1, keepdims=True)
            ref_weights = jnp.exp(ref_scores - ref_peak)
            ref_total = jnp.sum(ref_weights, axis=1, keepdims=True)
            ref_summed = jnp.dot(
                ref_weights.astype(jnp.bfloat16), rv_ref[...], preferred_element_type=jnp.float32
            )
            results.append((own, summed / t_new + ref_summed / ref_total))
        else:
            m_cur = jnp.where(picked, m_new, m_cur)
            t_cur = jnp.where(picked, t_new, t_cur)
            results.append((own, summed))
    merged = results[-1][1]
    for own, value in results[:-1]:
        merged = jnp.where(own, value, merged)
    if final:
        out_ref[...] = merged.astype(out_ref.dtype)
    else:
        acc_out[...] = merged

        @pl.when(step == 0)
        def _():
            m_out[...] = m_cur
            t_out[...] = t_cur

        @pl.when(step > 0)
        def _():
            m_out[...] = jnp.where((lane // 2) == step, m_cur, m_out[...])
            t_out[...] = jnp.where((lane // 2) == step, t_cur, t_out[...])


def absorb(queries, piece, bias, state, ref, final):
    rows, width = queries.shape
    blocks = width // LANES
    piece_keys, piece_values = piece
    count = piece_keys.shape[0]
    column = lambda j: (0, j)
    fixed = lambda j: (0, 0)
    in_specs = [
        pl.BlockSpec((rows, LANES), column),
        pl.BlockSpec((count, LANES), column),
        pl.BlockSpec((count, LANES), column),
        pl.BlockSpec((rows, count), fixed),
    ]
    operands = [queries, piece_keys, piece_values, bias]
    if state is not None:
        in_specs += [
            pl.BlockSpec((rows, LANES), fixed),
            pl.BlockSpec((rows, LANES), fixed),
            pl.BlockSpec((rows, LANES), column),
        ]
        operands += list(state)
    ref_rows = 0
    if final:
        ref_keys, ref_values = ref
        ref_rows = ref_keys.shape[0]
        in_specs += [pl.BlockSpec((ref_rows, LANES), column), pl.BlockSpec((ref_rows, LANES), column)]
        operands += [ref_keys, ref_values]
        out_specs = pl.BlockSpec((rows, LANES), column)
        out_shape = jax.ShapeDtypeStruct((rows, width), jnp.bfloat16)
    else:
        out_specs = (
            pl.BlockSpec((rows, LANES), fixed),
            pl.BlockSpec((rows, LANES), fixed),
            pl.BlockSpec((rows, LANES), column),
        )
        out_shape = (
            jax.ShapeDtypeStruct((rows, LANES), jnp.float32),
            jax.ShapeDtypeStruct((rows, LANES), jnp.float32),
            jax.ShapeDtypeStruct((rows, width), jnp.float32),
        )
    keys = count + ref_rows
    return pl.pallas_call(
        functools.partial(absorb_kernel, state is None, final),
        grid=(blocks,),
        in_specs=in_specs,
        out_specs=out_specs,
        out_shape=out_shape,
        compiler_params=pltpu.CompilerParams(
            dimension_semantics=("arbitrary",), vmem_limit_bytes=48 * 1024 * 1024
        ),
        cost_estimate=pl.CostEstimate(
            flops=8 * rows * keys * width,
            transcendentals=2 * rows * keys * HEADS,
            bytes_accessed=2 * (rows + 2 * keys) * width + 4 * rows * (count + 3 * width),
        ),
    )(*operands)


def key_bias(query_views, query_adjacent, positions, shard_rows, view_tok):
    key_rows = (positions[:, None] * shard_rows + jnp.arange(shard_rows, dtype=jnp.int32)[None, :]).reshape(-1)
    key_views = key_rows // view_tok
    keep = query_views[:, None] == key_views[None, :]
    for slot in range(ADJ):
        keep = keep | (query_adjacent[:, slot : slot + 1] == key_views[None, :].astype(jnp.float32))
    return jnp.where(keep, 0.0, -jnp.inf).astype(jnp.float32)


def body(queries, keys, values, ref_keys, ref_values, out_weight, adjacency, ref_source):
    shard_rows, width = queries.shape
    view_count = lax.axis_size("view")
    view_index = lax.axis_index("view")
    view_tok = shard_rows * view_count // VIEWS

    view_ids = jnp.arange(VIEWS, dtype=jnp.int32)
    query_views = (view_index * shard_rows + jnp.arange(shard_rows, dtype=jnp.int32)) // view_tok
    query_onehot = (query_views[:, None] == view_ids[None, :]).astype(jnp.float32)
    query_adjacent = jnp.dot(query_onehot, adjacency.astype(jnp.float32))

    def bias_for(*positions):
        return key_bias(query_views, query_adjacent, jnp.stack(positions), shard_rows, view_tok)

    own = (keys, values)
    if view_count == 4:
        across = lax.ppermute(own, "view", [(i, i ^ 2) for i in range(view_count)])
        near = lax.ppermute(own, "view", [(i, i ^ 1) for i in range(view_count)])
        far = lax.ppermute(across, "view", [(i, i ^ 1) for i in range(view_count)])
    ref_both = jnp.concatenate([ref_keys, ref_values], axis=1)
    ref_shared = gather_rows(tree_broadcast(ref_both, "mesh", ref_source[0]), "view")
    ref_all = (ref_shared[:, :width], ref_shared[:, width:])

    if view_count == 4:
        state = absorb(queries, own, bias_for(view_index), None, None, False)
        state = absorb(queries, near, bias_for(view_index ^ 1), state, None, False)
        state = absorb(queries, across, bias_for(view_index ^ 2), state, None, False)
        mixed = absorb(queries, far, bias_for(view_index ^ 3), state, ref_all, True)
    else:
        whole = lax.all_gather(own, "view", axis=0, tiled=True)
        mixed = absorb(queries, whole, bias_for(*range(view_count)), None, ref_all, True)
    return jnp.dot(mixed, out_weight, preferred_element_type=jnp.float32).astype(jnp.bfloat16)


def solution(mesh):
    return jax.shard_map(
        body,
        mesh=mesh,
        in_specs=(
            P(("mesh", "view"), None),
            P(("mesh", "view"), None),
            P(("mesh", "view"), None),
            P(("mesh", "view"), None),
            P(("mesh", "view"), None),
            P(),
            P("mesh", None),
            P(),
        ),
        out_specs=P(("mesh", "view"), None),
        check_vma=False,
    )
```

```python
import functools

import jax
import jax.numpy as jnp
from jax import lax
from jax.experimental import pallas as pl
from jax.experimental.pallas import tpu as pltpu
from jax.sharding import PartitionSpec as P

HEADS = 20
HEAD_DIM = 64
VIEWS = 6
ADJ = 3
SCALE = 0.125
LANES = 128


def tree_broadcast(value, axis, source):
    count = lax.axis_size(axis)
    index = lax.axis_index(axis)
    if count & (count - 1):
        kept = jnp.where(index == source, value, jnp.zeros_like(value))
        return lax.psum(kept, axis)
    distance = 1
    while distance < count:
        pairs = [(i, i ^ distance) for i in range(count)]
        received = lax.ppermute(value, axis, pairs)
        partner_has = ((index ^ distance) // distance) == (source // distance)
        value = jnp.where(partner_has, received, value)
        distance *= 2
    return value


def gather_rows(value, axis):
    count = lax.axis_size(axis)
    if count == 4:
        across = lax.ppermute(value, axis, [(i, i ^ 2) for i in range(count)])
        both = jnp.concatenate([value, across], axis=0)
        near = lax.ppermute(both, axis, [(i, i ^ 1) for i in range(count)])
        return jnp.concatenate([both, near], axis=0)
    return lax.all_gather(value, axis, axis=0, tiled=True)


def attention_kernel(piece_count, pairs, q_ref, *refs):
    key_refs = refs[:piece_count]
    value_refs = refs[piece_count : 2 * piece_count]
    bias_refs = refs[2 * piece_count : 3 * piece_count]
    rk_ref, rv_ref, out_ref = refs[3 * piece_count :]
    lane = lax.broadcasted_iota(jnp.int32, (1, LANES), 1)
    dims = (((1,), (1,)), ((), ()))
    for pair in range(pairs):
        cols = slice(pair * LANES, (pair + 1) * LANES)
        queries = q_ref[:, cols]
        results = []
        for head in range(LANES // HEAD_DIM):
            own = (lane // HEAD_DIM) == head
            q_head = jnp.where(own, queries, jnp.zeros_like(queries))
            scores = [
                lax.dot_general(q_head, key_refs[p][:, cols], dims, preferred_element_type=jnp.float32)
                * SCALE
                + bias_refs[p][...]
                for p in range(piece_count)
            ]
            peak = jnp.max(scores[0], axis=1, keepdims=True)
            for p in range(1, piece_count):
                peak = jnp.maximum(peak, jnp.max(scores[p], axis=1, keepdims=True))
            total = None
            summed = None
            for p in range(piece_count):
                weights = jnp.exp(scores[p] - peak)
                part_total = jnp.sum(weights, axis=1, keepdims=True)
                part = jnp.dot(
                    weights.astype(jnp.bfloat16), value_refs[p][:, cols], preferred_element_type=jnp.float32
                )
                total = part_total if total is None else total + part_total
                summed = part if summed is None else summed + part
            view_part = summed / total
            ref_scores = (
                lax.dot_general(q_head, rk_ref[:, cols], dims, preferred_element_type=jnp.float32) * SCALE
            )
            ref_peak = jnp.max(ref_scores, axis=1, keepdims=True)
            ref_weights = jnp.exp(ref_scores - ref_peak)
            ref_total = jnp.sum(ref_weights, axis=1, keepdims=True)
            ref_summed = jnp.dot(
                ref_weights.astype(jnp.bfloat16), rv_ref[:, cols], preferred_element_type=jnp.float32
            )
            results.append((own, view_part + ref_summed / ref_total))
        mixed = results[-1][1]
        for own, value in results[:-1]:
            mixed = jnp.where(own, value, mixed)
        out_ref[:, cols] = mixed.astype(out_ref.dtype)


def attention(queries, key_pieces, value_pieces, biases, ref_keys, ref_values, steps):
    rows, width = queries.shape
    span = width // steps
    column = lambda j: (0, j)
    fixed = lambda j: (0, 0)
    in_specs = [pl.BlockSpec((rows, span), column)]
    in_specs += [pl.BlockSpec((piece.shape[0], span), column) for piece in key_pieces]
    in_specs += [pl.BlockSpec((piece.shape[0], span), column) for piece in value_pieces]
    in_specs += [pl.BlockSpec(bias.shape, fixed) for bias in biases]
    in_specs += [pl.BlockSpec((ref_keys.shape[0], span), column)] * 2
    keys = sum(piece.shape[0] for piece in key_pieces) + ref_keys.shape[0]
    return pl.pallas_call(
        functools.partial(attention_kernel, len(key_pieces), span // LANES),
        grid=(steps,),
        in_specs=in_specs,
        out_specs=pl.BlockSpec((rows, span), column),
        out_shape=jax.ShapeDtypeStruct((rows, width), jnp.bfloat16),
        compiler_params=pltpu.CompilerParams(
            dimension_semantics=("arbitrary",), vmem_limit_bytes=48 * 1024 * 1024
        ),
        cost_estimate=pl.CostEstimate(
            flops=8 * rows * keys * width,
            transcendentals=2 * rows * keys * HEADS,
            bytes_accessed=2 * (2 * rows + 2 * keys) * width + 4 * rows * keys,
        ),
    )(queries, *key_pieces, *value_pieces, *biases, ref_keys, ref_values)


def key_bias(query_views, query_adjacent, position, rows, shard_rows, view_tok):
    key_rows = position * shard_rows + jnp.arange(rows, dtype=jnp.int32)
    key_views = key_rows // view_tok
    keep = query_views[:, None] == key_views[None, :]
    for slot in range(ADJ):
        keep = keep | (query_adjacent[:, slot : slot + 1] == key_views[None, :].astype(jnp.float32))
    return jnp.where(keep, 0.0, -jnp.inf).astype(jnp.float32)


def body(queries, keys, values, ref_keys, ref_values, out_weight, adjacency, ref_source):
    shard_rows, width = queries.shape
    view_count = lax.axis_size("view")
    view_index = lax.axis_index("view")
    view_tok = shard_rows * view_count // VIEWS

    if view_count == 4:
        across = lax.ppermute((keys, values), "view", [(i, i ^ 2) for i in range(view_count)])
        near = lax.ppermute((keys, values), "view", [(i, i ^ 1) for i in range(view_count)])
        far = lax.ppermute(across, "view", [(i, i ^ 1) for i in range(view_count)])
        pieces = [(keys, values), near, across, far]
        positions = [view_index, view_index ^ 1, view_index ^ 2, view_index ^ 3]
    else:
        pieces = [lax.all_gather((keys, values), "view", axis=0, tiled=True)]
        positions = [jnp.zeros((), jnp.int32)]

    ref_both = jnp.concatenate([ref_keys, ref_values], axis=1)
    ref_all = gather_rows(tree_broadcast(ref_both, "mesh", ref_source[0]), "view")

    view_ids = jnp.arange(VIEWS, dtype=jnp.int32)
    query_views = (view_index * shard_rows + jnp.arange(shard_rows, dtype=jnp.int32)) // view_tok
    query_onehot = (query_views[:, None] == view_ids[None, :]).astype(jnp.float32)
    query_adjacent = jnp.dot(query_onehot, adjacency.astype(jnp.float32))
    biases = [
        key_bias(query_views, query_adjacent, position, piece[0].shape[0], shard_rows, view_tok)
        for piece, position in zip(pieces, positions)
    ]

    mixed = attention(
        queries,
        [piece[0] for piece in pieces],
        [piece[1] for piece in pieces],
        biases,
        ref_all[:, :width],
        ref_all[:, width:],
        2,
    )
    return jnp.dot(mixed, out_weight, preferred_element_type=jnp.float32).astype(jnp.bfloat16)


def solution(mesh):
    return jax.shard_map(
        body,
        mesh=mesh,
        in_specs=(
            P(("mesh", "view"), None),
            P(("mesh", "view"), None),
            P(("mesh", "view"), None),
            P(("mesh", "view"), None),
            P(("mesh", "view"), None),
            P(),
            P("mesh", None),
            P(),
        ),
        out_specs=P(("mesh", "view"), None),
        check_vma=False,
    )
```

```python
import functools

import jax
import jax.numpy as jnp
from jax import lax
from jax.experimental import pallas as pl
from jax.experimental.pallas import tpu as pltpu
from jax.sharding import PartitionSpec as P

HEADS = 20
HEAD_DIM = 64
VIEWS = 6
ADJ = 3
SCALE = 0.125
LANES = 128


def tree_broadcast(value, axis, source):
    count = lax.axis_size(axis)
    index = lax.axis_index(axis)
    if count & (count - 1) or count < 4:
        kept = jnp.where(index == source, value, jnp.zeros_like(value))
        return lax.psum(kept, axis)
    gathered = value
    for distance in (1, 2, 3):
        received = lax.ppermute(value, axis, [(i, i ^ distance) for i in range(count)])
        gathered = jnp.where((index ^ distance) == source, received, gathered)
    value = gathered
    distance = 4
    while distance < count:
        received = lax.ppermute(value, axis, [(i, i ^ distance) for i in range(count)])
        partner_has = ((index ^ distance) // distance) == (source // distance)
        value = jnp.where(partner_has, received, value)
        distance *= 2
    return value


def gather_rows(value, axis):
    count = lax.axis_size(axis)
    if count == 4:
        across = lax.ppermute(value, axis, [(i, i ^ 2) for i in range(count)])
        both = jnp.concatenate([value, across], axis=0)
        near = lax.ppermute(both, axis, [(i, i ^ 1) for i in range(count)])
        return jnp.concatenate([both, near], axis=0)
    return lax.all_gather(value, axis, axis=0, tiled=True)


def attention_kernel(piece_count, pairs, q_ref, *refs):
    key_refs = refs[:piece_count]
    value_refs = refs[piece_count : 2 * piece_count]
    bias_refs = refs[2 * piece_count : 3 * piece_count]
    rk_ref, rv_ref, out_ref = refs[3 * piece_count :]
    lane = lax.broadcasted_iota(jnp.int32, (1, LANES), 1)
    dims = (((1,), (1,)), ((), ()))
    for pair in range(pairs):
        cols = slice(pair * LANES, (pair + 1) * LANES)
        queries = q_ref[:, cols]
        results = []
        for head in range(LANES // HEAD_DIM):
            own = (lane // HEAD_DIM) == head
            q_head = jnp.where(own, queries, jnp.zeros_like(queries))
            scores = [
                lax.dot_general(q_head, key_refs[p][:, cols], dims, preferred_element_type=jnp.float32)
                * SCALE
                + bias_refs[p][...]
                for p in range(piece_count)
            ]
            peak = jnp.max(scores[0], axis=1, keepdims=True)
            for p in range(1, piece_count):
                peak = jnp.maximum(peak, jnp.max(scores[p], axis=1, keepdims=True))
            total = None
            summed = None
            for p in range(piece_count):
                weights = jnp.exp(scores[p] - peak)
                part_total = jnp.sum(weights, axis=1, keepdims=True)
                part = jnp.dot(
                    weights.astype(jnp.bfloat16), value_refs[p][:, cols], preferred_element_type=jnp.float32
                )
                total = part_total if total is None else total + part_total
                summed = part if summed is None else summed + part
            view_part = summed / total
            ref_scores = (
                lax.dot_general(q_head, rk_ref[:, cols], dims, preferred_element_type=jnp.float32) * SCALE
            )
            ref_peak = jnp.max(ref_scores, axis=1, keepdims=True)
            ref_weights = jnp.exp(ref_scores - ref_peak)
            ref_total = jnp.sum(ref_weights, axis=1, keepdims=True)
            ref_summed = jnp.dot(
                ref_weights.astype(jnp.bfloat16), rv_ref[:, cols], preferred_element_type=jnp.float32
            )
            results.append((own, view_part + ref_summed / ref_total))
        mixed = results[-1][1]
        for own, value in results[:-1]:
            mixed = jnp.where(own, value, mixed)
        out_ref[:, cols] = mixed.astype(out_ref.dtype)


def attention(queries, key_pieces, value_pieces, biases, ref_keys, ref_values, steps):
    rows, width = queries.shape
    span = width // steps
    column = lambda j: (0, j)
    fixed = lambda j: (0, 0)
    in_specs = [pl.BlockSpec((rows, span), column)]
    in_specs += [pl.BlockSpec((piece.shape[0], span), column) for piece in key_pieces]
    in_specs += [pl.BlockSpec((piece.shape[0], span), column) for piece in value_pieces]
    in_specs += [pl.BlockSpec(bias.shape, fixed) for bias in biases]
    in_specs += [pl.BlockSpec((ref_keys.shape[0], span), column)] * 2
    keys = sum(piece.shape[0] for piece in key_pieces) + ref_keys.shape[0]
    return pl.pallas_call(
        functools.partial(attention_kernel, len(key_pieces), span // LANES),
        grid=(steps,),
        in_specs=in_specs,
        out_specs=pl.BlockSpec((rows, span), column),
        out_shape=jax.ShapeDtypeStruct((rows, width), jnp.bfloat16),
        compiler_params=pltpu.CompilerParams(
            dimension_semantics=("arbitrary",), vmem_limit_bytes=48 * 1024 * 1024
        ),
        cost_estimate=pl.CostEstimate(
            flops=8 * rows * keys * width,
            transcendentals=2 * rows * keys * HEADS,
            bytes_accessed=2 * (2 * rows + 2 * keys) * width + 4 * rows * keys,
        ),
    )(queries, *key_pieces, *value_pieces, *biases, ref_keys, ref_values)


def key_bias(query_views, query_adjacent, position, rows, shard_rows, view_tok):
    key_rows = position * shard_rows + jnp.arange(rows, dtype=jnp.int32)
    key_views = key_rows // view_tok
    keep = query_views[:, None] == key_views[None, :]
    for slot in range(ADJ):
        keep = keep | (query_adjacent[:, slot : slot + 1] == key_views[None, :].astype(jnp.float32))
    return jnp.where(keep, 0.0, -jnp.inf).astype(jnp.float32)


def body(queries, keys, values, ref_keys, ref_values, out_weight, adjacency, ref_source):
    shard_rows, width = queries.shape
    view_count = lax.axis_size("view")
    view_index = lax.axis_index("view")
    view_tok = shard_rows * view_count // VIEWS

    if view_count == 4:
        across = lax.ppermute((keys, values), "view", [(i, i ^ 2) for i in range(view_count)])
        near = lax.ppermute((keys, values), "view", [(i, i ^ 1) for i in range(view_count)])
        far = lax.ppermute(across, "view", [(i, i ^ 1) for i in range(view_count)])
        pieces = [(keys, values), near, across, far]
        positions = [view_index, view_index ^ 1, view_index ^ 2, view_index ^ 3]
    else:
        pieces = [lax.all_gather((keys, values), "view", axis=0, tiled=True)]
        positions = [jnp.zeros((), jnp.int32)]

    ref_both = jnp.concatenate([ref_keys, ref_values], axis=1)
    ref_all = gather_rows(tree_broadcast(ref_both, "mesh", ref_source[0]), "view")

    view_ids = jnp.arange(VIEWS, dtype=jnp.int32)
    query_views = (view_index * shard_rows + jnp.arange(shard_rows, dtype=jnp.int32)) // view_tok
    query_onehot = (query_views[:, None] == view_ids[None, :]).astype(jnp.float32)
    query_adjacent = jnp.dot(query_onehot, adjacency.astype(jnp.float32))
    biases = [
        key_bias(query_views, query_adjacent, position, piece[0].shape[0], shard_rows, view_tok)
        for piece, position in zip(pieces, positions)
    ]

    mixed = attention(
        queries,
        [piece[0] for piece in pieces],
        [piece[1] for piece in pieces],
        biases,
        ref_all[:, :width],
        ref_all[:, width:],
        2,
    )
    return jnp.dot(mixed, out_weight, preferred_element_type=jnp.float32).astype(jnp.bfloat16)


def solution(mesh):
    return jax.shard_map(
        body,
        mesh=mesh,
        in_specs=(
            P(("mesh", "view"), None),
            P(("mesh", "view"), None),
            P(("mesh", "view"), None),
            P(("mesh", "view"), None),
            P(("mesh", "view"), None),
            P(),
            P("mesh", None),
            P(),
        ),
        out_specs=P(("mesh", "view"), None),
        check_vma=False,
    )
```

```python
import functools

import jax
import jax.numpy as jnp
from jax import lax
from jax.experimental import pallas as pl
from jax.experimental.pallas import tpu as pltpu
from jax.sharding import PartitionSpec as P

HEADS = 20
HEAD_DIM = 64
VIEWS = 6
ADJ = 3
SCALE = 0.125
LANES = 128


def tree_broadcast(value, axis, source):
    count = lax.axis_size(axis)
    index = lax.axis_index(axis)
    if count & (count - 1):
        kept = jnp.where(index == source, value, jnp.zeros_like(value))
        return lax.psum(kept, axis)
    distance = 1
    while distance < count:
        pairs = [(i, i ^ distance) for i in range(count)]
        received = lax.ppermute(value, axis, pairs)
        partner_has = ((index ^ distance) // distance) == (source // distance)
        value = jnp.where(partner_has, received, value)
        distance *= 2
    return value


def gather_rows(value, axis):
    count = lax.axis_size(axis)
    if count == 4:
        across = lax.ppermute(value, axis, [(i, i ^ 2) for i in range(count)])
        both = jnp.concatenate([value, across], axis=0)
        near = lax.ppermute(both, axis, [(i, i ^ 1) for i in range(count)])
        return jnp.concatenate([both, near], axis=0)
    return lax.all_gather(value, axis, axis=0, tiled=True)


def attention_kernel(piece_count, pairs, q_ref, *refs):
    key_refs = refs[:piece_count]
    value_refs = refs[piece_count : 2 * piece_count]
    bias_refs = refs[2 * piece_count : 3 * piece_count]
    rk_ref, rv_ref, out_ref = refs[3 * piece_count :]
    lane = lax.broadcasted_iota(jnp.int32, (1, LANES), 1)
    dims = (((1,), (1,)), ((), ()))
    for pair in range(pairs):
        cols = slice(pair * LANES, (pair + 1) * LANES)
        queries = q_ref[:, cols]
        results = []
        for head in range(LANES // HEAD_DIM):
            own = (lane // HEAD_DIM) == head
            q_head = jnp.where(own, queries, jnp.zeros_like(queries))
            scores = [
                lax.dot_general(q_head, key_refs[p][:, cols], dims, preferred_element_type=jnp.float32)
                * SCALE
                + bias_refs[p][...]
                for p in range(piece_count)
            ]
            peak = jnp.max(scores[0], axis=1, keepdims=True)
            for p in range(1, piece_count):
                peak = jnp.maximum(peak, jnp.max(scores[p], axis=1, keepdims=True))
            total = None
            summed = None
            for p in range(piece_count):
                weights = jnp.exp(scores[p] - peak)
                part_total = jnp.sum(weights, axis=1, keepdims=True)
                part = jnp.dot(
                    weights.astype(jnp.bfloat16), value_refs[p][:, cols], preferred_element_type=jnp.float32
                )
                total = part_total if total is None else total + part_total
                summed = part if summed is None else summed + part
            view_part = summed / total
            ref_scores = (
                lax.dot_general(q_head, rk_ref[:, cols], dims, preferred_element_type=jnp.float32) * SCALE
            )
            ref_peak = jnp.max(ref_scores, axis=1, keepdims=True)
            ref_weights = jnp.exp(ref_scores - ref_peak)
            ref_total = jnp.sum(ref_weights, axis=1, keepdims=True)
            ref_summed = jnp.dot(
                ref_weights.astype(jnp.bfloat16), rv_ref[:, cols], preferred_element_type=jnp.float32
            )
            results.append((own, view_part + ref_summed / ref_total))
        mixed = results[-1][1]
        for own, value in results[:-1]:
            mixed = jnp.where(own, value, mixed)
        out_ref[:, cols] = mixed.astype(out_ref.dtype)


def attention(queries, key_pieces, value_pieces, biases, ref_keys, ref_values, steps):
    rows, width = queries.shape
    span = width // steps
    column = lambda j: (0, j)
    fixed = lambda j: (0, 0)
    in_specs = [pl.BlockSpec((rows, span), column)]
    in_specs += [pl.BlockSpec((piece.shape[0], span), column) for piece in key_pieces]
    in_specs += [pl.BlockSpec((piece.shape[0], span), column) for piece in value_pieces]
    in_specs += [pl.BlockSpec(bias.shape, fixed) for bias in biases]
    in_specs += [pl.BlockSpec((ref_keys.shape[0], span), column)] * 2
    keys = sum(piece.shape[0] for piece in key_pieces) + ref_keys.shape[0]
    return pl.pallas_call(
        functools.partial(attention_kernel, len(key_pieces), span // LANES),
        grid=(steps,),
        in_specs=in_specs,
        out_specs=pl.BlockSpec((rows, span), column),
        out_shape=jax.ShapeDtypeStruct((rows, width), jnp.bfloat16),
        compiler_params=pltpu.CompilerParams(
            dimension_semantics=("arbitrary",), vmem_limit_bytes=48 * 1024 * 1024
        ),
        cost_estimate=pl.CostEstimate(
            flops=8 * rows * keys * width,
            transcendentals=2 * rows * keys * HEADS,
            bytes_accessed=2 * (2 * rows + 2 * keys) * width + 4 * rows * keys,
        ),
    )(queries, *key_pieces, *value_pieces, *biases, ref_keys, ref_values)


def key_bias(query_views, query_adjacent, position, rows, shard_rows, view_tok):
    key_rows = position * shard_rows + jnp.arange(rows, dtype=jnp.int32)
    key_views = key_rows // view_tok
    keep = query_views[:, None] == key_views[None, :]
    for slot in range(ADJ):
        keep = keep | (query_adjacent[:, slot : slot + 1] == key_views[None, :].astype(jnp.float32))
    return jnp.where(keep, 0.0, -jnp.inf).astype(jnp.float32)


def body(queries, keys, values, ref_keys, ref_values, out_weight, adjacency, ref_source):
    shard_rows, width = queries.shape
    view_count = lax.axis_size("view")
    view_index = lax.axis_index("view")
    view_tok = shard_rows * view_count // VIEWS

    ref_both = jnp.concatenate([ref_keys, ref_values], axis=1)
    if view_count == 4:
        ref_across = lax.ppermute(ref_both, "view", [(i, i ^ 2) for i in range(view_count)])
        ref_half = jnp.concatenate([ref_both, ref_across], axis=0)
        ref_shared = tree_broadcast(ref_half, "mesh", ref_source[0])
        ref_near = lax.ppermute(ref_shared, "view", [(i, i ^ 1) for i in range(view_count)])
        ref_all = jnp.concatenate([ref_shared, ref_near], axis=0)
    else:
        ref_all = gather_rows(tree_broadcast(ref_both, "mesh", ref_source[0]), "view")

    if view_count == 4:
        across = lax.ppermute((keys, values), "view", [(i, i ^ 2) for i in range(view_count)])
        near = lax.ppermute((keys, values), "view", [(i, i ^ 1) for i in range(view_count)])
        far = lax.ppermute(across, "view", [(i, i ^ 1) for i in range(view_count)])
        pieces = [(keys, values), near, across, far]
        positions = [view_index, view_index ^ 1, view_index ^ 2, view_index ^ 3]
    else:
        pieces = [lax.all_gather((keys, values), "view", axis=0, tiled=True)]
        positions = [jnp.zeros((), jnp.int32)]


    view_ids = jnp.arange(VIEWS, dtype=jnp.int32)
    query_views = (view_index * shard_rows + jnp.arange(shard_rows, dtype=jnp.int32)) // view_tok
    query_onehot = (query_views[:, None] == view_ids[None, :]).astype(jnp.float32)
    query_adjacent = jnp.dot(query_onehot, adjacency.astype(jnp.float32))
    biases = [
        key_bias(query_views, query_adjacent, position, piece[0].shape[0], shard_rows, view_tok)
        for piece, position in zip(pieces, positions)
    ]

    mixed = attention(
        queries,
        [piece[0] for piece in pieces],
        [piece[1] for piece in pieces],
        biases,
        ref_all[:, :width],
        ref_all[:, width:],
        2,
    )
    return jnp.dot(mixed, out_weight, preferred_element_type=jnp.float32).astype(jnp.bfloat16)


def solution(mesh):
    return jax.shard_map(
        body,
        mesh=mesh,
        in_specs=(
            P(("mesh", "view"), None),
            P(("mesh", "view"), None),
            P(("mesh", "view"), None),
            P(("mesh", "view"), None),
            P(("mesh", "view"), None),
            P(),
            P("mesh", None),
            P(),
        ),
        out_specs=P(("mesh", "view"), None),
        check_vma=False,
    )
```

```python
import functools

import jax
import jax.numpy as jnp
from jax import lax
from jax.experimental import pallas as pl
from jax.experimental.pallas import tpu as pltpu
from jax.sharding import PartitionSpec as P

HEADS = 20
HEAD_DIM = 64
VIEWS = 6
ADJ = 3
SCALE = 0.125
LANES = 128


def tree_broadcast(value, axis, source):
    count = lax.axis_size(axis)
    index = lax.axis_index(axis)
    if count & (count - 1):
        kept = jnp.where(index == source, value, jnp.zeros_like(value))
        return lax.psum(kept, axis)
    distance = count // 2
    while distance >= 1:
        pairs = [(i, i ^ distance) for i in range(count)]
        received = lax.ppermute(value, axis, pairs)
        partner_has = ((index ^ distance) % (2 * distance)) == (source % (2 * distance))
        value = jnp.where(partner_has, received, value)
        distance //= 2
    return value


def gather_rows(value, axis):
    count = lax.axis_size(axis)
    if count == 4:
        across = lax.ppermute(value, axis, [(i, i ^ 2) for i in range(count)])
        both = jnp.concatenate([value, across], axis=0)
        near = lax.ppermute(both, axis, [(i, i ^ 1) for i in range(count)])
        return jnp.concatenate([both, near], axis=0)
    return lax.all_gather(value, axis, axis=0, tiled=True)


def attention_kernel(piece_count, pairs, q_ref, *refs):
    key_refs = refs[:piece_count]
    value_refs = refs[piece_count : 2 * piece_count]
    bias_refs = refs[2 * piece_count : 3 * piece_count]
    rk_ref, rv_ref, out_ref = refs[3 * piece_count :]
    lane = lax.broadcasted_iota(jnp.int32, (1, LANES), 1)
    dims = (((1,), (1,)), ((), ()))
    for pair in range(pairs):
        cols = slice(pair * LANES, (pair + 1) * LANES)
        queries = q_ref[:, cols]
        results = []
        for head in range(LANES // HEAD_DIM):
            own = (lane // HEAD_DIM) == head
            q_head = jnp.where(own, queries, jnp.zeros_like(queries))
            scores = [
                lax.dot_general(q_head, key_refs[p][:, cols], dims, preferred_element_type=jnp.float32)
                * SCALE
                + bias_refs[p][...]
                for p in range(piece_count)
            ]
            peak = jnp.max(scores[0], axis=1, keepdims=True)
            for p in range(1, piece_count):
                peak = jnp.maximum(peak, jnp.max(scores[p], axis=1, keepdims=True))
            total = None
            summed = None
            for p in range(piece_count):
                weights = jnp.exp(scores[p] - peak)
                part_total = jnp.sum(weights, axis=1, keepdims=True)
                part = jnp.dot(
                    weights.astype(jnp.bfloat16), value_refs[p][:, cols], preferred_element_type=jnp.float32
                )
                total = part_total if total is None else total + part_total
                summed = part if summed is None else summed + part
            view_part = summed / total
            ref_scores = (
                lax.dot_general(q_head, rk_ref[:, cols], dims, preferred_element_type=jnp.float32) * SCALE
            )
            ref_peak = jnp.max(ref_scores, axis=1, keepdims=True)
            ref_weights = jnp.exp(ref_scores - ref_peak)
            ref_total = jnp.sum(ref_weights, axis=1, keepdims=True)
            ref_summed = jnp.dot(
                ref_weights.astype(jnp.bfloat16), rv_ref[:, cols], preferred_element_type=jnp.float32
            )
            results.append((own, view_part + ref_summed / ref_total))
        mixed = results[-1][1]
        for own, value in results[:-1]:
            mixed = jnp.where(own, value, mixed)
        out_ref[:, cols] = mixed.astype(out_ref.dtype)


def attention(queries, key_pieces, value_pieces, biases, ref_keys, ref_values, steps):
    rows, width = queries.shape
    span = width // steps
    column = lambda j: (0, j)
    fixed = lambda j: (0, 0)
    in_specs = [pl.BlockSpec((rows, span), column)]
    in_specs += [pl.BlockSpec((piece.shape[0], span), column) for piece in key_pieces]
    in_specs += [pl.BlockSpec((piece.shape[0], span), column) for piece in value_pieces]
    in_specs += [pl.BlockSpec(bias.shape, fixed) for bias in biases]
    in_specs += [pl.BlockSpec((ref_keys.shape[0], span), column)] * 2
    keys = sum(piece.shape[0] for piece in key_pieces) + ref_keys.shape[0]
    return pl.pallas_call(
        functools.partial(attention_kernel, len(key_pieces), span // LANES),
        grid=(steps,),
        in_specs=in_specs,
        out_specs=pl.BlockSpec((rows, span), column),
        out_shape=jax.ShapeDtypeStruct((rows, width), jnp.bfloat16),
        compiler_params=pltpu.CompilerParams(
            dimension_semantics=("arbitrary",), vmem_limit_bytes=48 * 1024 * 1024
        ),
        cost_estimate=pl.CostEstimate(
            flops=8 * rows * keys * width,
            transcendentals=2 * rows * keys * HEADS,
            bytes_accessed=2 * (2 * rows + 2 * keys) * width + 4 * rows * keys,
        ),
    )(queries, *key_pieces, *value_pieces, *biases, ref_keys, ref_values)


def key_bias(query_views, query_adjacent, position, rows, shard_rows, view_tok):
    key_rows = position * shard_rows + jnp.arange(rows, dtype=jnp.int32)
    key_views = key_rows // view_tok
    keep = query_views[:, None] == key_views[None, :]
    for slot in range(ADJ):
        keep = keep | (query_adjacent[:, slot : slot + 1] == key_views[None, :].astype(jnp.float32))
    return jnp.where(keep, 0.0, -jnp.inf).astype(jnp.float32)


def body(queries, keys, values, ref_keys, ref_values, out_weight, adjacency, ref_source):
    shard_rows, width = queries.shape
    view_count = lax.axis_size("view")
    view_index = lax.axis_index("view")
    view_tok = shard_rows * view_count // VIEWS

    if view_count == 4:
        across = lax.ppermute((keys, values), "view", [(i, i ^ 2) for i in range(view_count)])
        near = lax.ppermute((keys, values), "view", [(i, i ^ 1) for i in range(view_count)])
        far = lax.ppermute(across, "view", [(i, i ^ 1) for i in range(view_count)])
        pieces = [(keys, values), near, across, far]
        positions = [view_index, view_index ^ 1, view_index ^ 2, view_index ^ 3]
    else:
        pieces = [lax.all_gather((keys, values), "view", axis=0, tiled=True)]
        positions = [jnp.zeros((), jnp.int32)]

    ref_both = jnp.concatenate([ref_keys, ref_values], axis=1)
    ref_all = gather_rows(tree_broadcast(ref_both, "mesh", ref_source[0]), "view")

    view_ids = jnp.arange(VIEWS, dtype=jnp.int32)
    query_views = (view_index * shard_rows + jnp.arange(shard_rows, dtype=jnp.int32)) // view_tok
    query_onehot = (query_views[:, None] == view_ids[None, :]).astype(jnp.float32)
    query_adjacent = jnp.dot(query_onehot, adjacency.astype(jnp.float32))
    biases = [
        key_bias(query_views, query_adjacent, position, piece[0].shape[0], shard_rows, view_tok)
        for piece, position in zip(pieces, positions)
    ]

    mixed = attention(
        queries,
        [piece[0] for piece in pieces],
        [piece[1] for piece in pieces],
        biases,
        ref_all[:, :width],
        ref_all[:, width:],
        2,
    )
    return jnp.dot(mixed, out_weight, preferred_element_type=jnp.float32).astype(jnp.bfloat16)


def solution(mesh):
    return jax.shard_map(
        body,
        mesh=mesh,
        in_specs=(
            P(("mesh", "view"), None),
            P(("mesh", "view"), None),
            P(("mesh", "view"), None),
            P(("mesh", "view"), None),
            P(("mesh", "view"), None),
            P(),
            P("mesh", None),
            P(),
        ),
        out_specs=P(("mesh", "view"), None),
        check_vma=False,
    )
```

```python
import functools

import jax
import jax.numpy as jnp
from jax import lax
from jax.experimental import pallas as pl
from jax.experimental.pallas import tpu as pltpu
from jax.sharding import PartitionSpec as P

HEADS = 20
HEAD_DIM = 64
VIEWS = 6
ADJ = 3
SCALE = 0.125
LANES = 128


def tree_broadcast(value, axis, source):
    count = lax.axis_size(axis)
    index = lax.axis_index(axis)
    if count & (count - 1):
        kept = jnp.where(index == source, value, jnp.zeros_like(value))
        return lax.psum(kept, axis)
    distance = 1
    while distance < count:
        pairs = [(i, i ^ distance) for i in range(count)]
        received = lax.ppermute(value, axis, pairs)
        partner_has = ((index ^ distance) // distance) == (source // distance)
        value = jnp.where(partner_has, received, value)
        distance *= 2
    return value


def gather_rows(value, axis):
    count = lax.axis_size(axis)
    if count == 4:
        across = lax.ppermute(value, axis, [(i, i ^ 2) for i in range(count)])
        both = jnp.concatenate([value, across], axis=0)
        near = lax.ppermute(both, axis, [(i, i ^ 1) for i in range(count)])
        return jnp.concatenate([both, near], axis=0)
    return lax.all_gather(value, axis, axis=0, tiled=True)


def attention_kernel(piece_count, pairs, has_state, final, q_ref, *refs):
    key_refs = refs[:piece_count]
    value_refs = refs[piece_count : 2 * piece_count]
    bias_refs = refs[2 * piece_count : 3 * piece_count]
    rest = list(refs[3 * piece_count :])
    if has_state:
        m_in, t_in, acc_in = rest[:3]
        rest = rest[3:]
    if final:
        rk_ref, rv_ref, out_ref = rest
    else:
        m_out, t_out, acc_out = rest
    step = pl.program_id(0)
    rows = q_ref.shape[0]
    lane = lax.broadcasted_iota(jnp.int32, (1, LANES), 1)
    dims = (((1,), (1,)), ((), ()))
    per_pair = LANES // HEAD_DIM
    if not final:

        @pl.when(step == 0)
        def _():
            m_out[...] = jnp.zeros((rows, LANES), jnp.float32)
            t_out[...] = jnp.zeros((rows, LANES), jnp.float32)

    if has_state:
        m_state = m_in[...]
        t_state = t_in[...]
    for pair in range(pairs):
        cols = slice(pair * LANES, (pair + 1) * LANES)
        queries = q_ref[:, cols]
        results = []
        for head in range(per_pair):
            own = (lane // HEAD_DIM) == head
            picked = lane == (step * pairs + pair) * per_pair + head
            q_head = jnp.where(own, queries, jnp.zeros_like(queries))
            scores = [
                lax.dot_general(q_head, key_refs[p][:, cols], dims, preferred_element_type=jnp.float32)
                * SCALE
                + bias_refs[p][...]
                for p in range(piece_count)
            ]
            peak = jnp.full((rows, 1), -1e30, jnp.float32)
            for p in range(piece_count):
                peak = jnp.maximum(peak, jnp.max(scores[p], axis=1, keepdims=True))
            if has_state:
                m_old = jnp.sum(jnp.where(picked, m_state, 0.0), axis=1, keepdims=True)
                t_old = jnp.sum(jnp.where(picked, t_state, 0.0), axis=1, keepdims=True)
                peak = jnp.maximum(peak, m_old)
                alpha = jnp.exp(m_old - peak)
            total = None
            summed = None
            for p in range(piece_count):
                weights = jnp.exp(scores[p] - peak)
                part_total = jnp.sum(weights, axis=1, keepdims=True)
                part = jnp.dot(
                    weights.astype(jnp.bfloat16), value_refs[p][:, cols], preferred_element_type=jnp.float32
                )
                total = part_total if total is None else total + part_total
                summed = part if summed is None else summed + part
            if has_state:
                total = alpha * t_old + total
                summed = alpha * acc_in[:, cols] + summed
            if final:
                ref_scores = (
                    lax.dot_general(q_head, rk_ref[:, cols], dims, preferred_element_type=jnp.float32)
                    * SCALE
                )
                ref_peak = jnp.max(ref_scores, axis=1, keepdims=True)
                ref_weights = jnp.exp(ref_scores - ref_peak)
                ref_total = jnp.sum(ref_weights, axis=1, keepdims=True)
                ref_summed = jnp.dot(
                    ref_weights.astype(jnp.bfloat16), rv_ref[:, cols], preferred_element_type=jnp.float32
                )
                results.append((own, summed / total + ref_summed / ref_total))
            else:
                m_out[...] = jnp.where(picked, peak, m_out[...])
                t_out[...] = jnp.where(picked, total, t_out[...])
                results.append((own, summed))
        merged = results[-1][1]
        for own, value in results[:-1]:
            merged = jnp.where(own, value, merged)
        if final:
            out_ref[:, cols] = merged.astype(out_ref.dtype)
        else:
            acc_out[:, cols] = merged


def attention(queries, key_pieces, value_pieces, biases, state, ref, steps):
    rows, width = queries.shape
    span = width // steps
    column = lambda j: (0, j)
    fixed = lambda j: (0, 0)
    in_specs = [pl.BlockSpec((rows, span), column)]
    in_specs += [pl.BlockSpec((piece.shape[0], span), column) for piece in key_pieces]
    in_specs += [pl.BlockSpec((piece.shape[0], span), column) for piece in value_pieces]
    in_specs += [pl.BlockSpec(bias.shape, fixed) for bias in biases]
    operands = [queries, *key_pieces, *value_pieces, *biases]
    keys = sum(piece.shape[0] for piece in key_pieces)
    if state is not None:
        in_specs += [pl.BlockSpec((rows, LANES), fixed)] * 2 + [pl.BlockSpec((rows, span), column)]
        operands += list(state)
    final = ref is not None
    if final:
        ref_keys, ref_values = ref
        keys += ref_keys.shape[0]
        in_specs += [pl.BlockSpec((ref_keys.shape[0], span), column)] * 2
        operands += [ref_keys, ref_values]
        out_specs = pl.BlockSpec((rows, span), column)
        out_shape = jax.ShapeDtypeStruct((rows, width), jnp.bfloat16)
    else:
        out_specs = (
            pl.BlockSpec((rows, LANES), fixed),
            pl.BlockSpec((rows, LANES), fixed),
            pl.BlockSpec((rows, span), column),
        )
        out_shape = (
            jax.ShapeDtypeStruct((rows, LANES), jnp.float32),
            jax.ShapeDtypeStruct((rows, LANES), jnp.float32),
            jax.ShapeDtypeStruct((rows, width), jnp.float32),
        )
    return pl.pallas_call(
        functools.partial(attention_kernel, len(key_pieces), span // LANES, state is not None, final),
        grid=(steps,),
        in_specs=in_specs,
        out_specs=out_specs,
        out_shape=out_shape,
        compiler_params=pltpu.CompilerParams(
            dimension_semantics=("arbitrary",), vmem_limit_bytes=48 * 1024 * 1024
        ),
        cost_estimate=pl.CostEstimate(
            flops=8 * rows * keys * width,
            transcendentals=2 * rows * keys * HEADS,
            bytes_accessed=2 * (2 * rows + 2 * keys) * width + 4 * rows * (keys + width),
        ),
    )(*operands)


def key_bias(query_views, query_adjacent, position, rows, shard_rows, view_tok):
    key_rows = position * shard_rows + jnp.arange(rows, dtype=jnp.int32)
    key_views = key_rows // view_tok
    keep = query_views[:, None] == key_views[None, :]
    for slot in range(ADJ):
        keep = keep | (query_adjacent[:, slot : slot + 1] == key_views[None, :].astype(jnp.float32))
    return jnp.where(keep, 0.0, -jnp.inf).astype(jnp.float32)


def body(queries, keys, values, ref_keys, ref_values, out_weight, adjacency, ref_source):
    shard_rows, width = queries.shape
    view_count = lax.axis_size("view")
    view_index = lax.axis_index("view")
    view_tok = shard_rows * view_count // VIEWS

    if view_count == 4:
        across = lax.ppermute((keys, values), "view", [(i, i ^ 2) for i in range(view_count)])
        near = lax.ppermute((keys, values), "view", [(i, i ^ 1) for i in range(view_count)])
        far = lax.ppermute(across, "view", [(i, i ^ 1) for i in range(view_count)])
        pieces = [(keys, values), near, across, far]
        positions = [view_index, view_index ^ 1, view_index ^ 2, view_index ^ 3]
    else:
        pieces = [lax.all_gather((keys, values), "view", axis=0, tiled=True)]
        positions = [jnp.zeros((), jnp.int32)]

    ref_both = jnp.concatenate([ref_keys, ref_values], axis=1)
    ref_all = gather_rows(tree_broadcast(ref_both, "mesh", ref_source[0]), "view")

    view_ids = jnp.arange(VIEWS, dtype=jnp.int32)
    query_views = (view_index * shard_rows + jnp.arange(shard_rows, dtype=jnp.int32)) // view_tok
    query_onehot = (query_views[:, None] == view_ids[None, :]).astype(jnp.float32)
    query_adjacent = jnp.dot(query_onehot, adjacency.astype(jnp.float32))
    biases = [
        key_bias(query_views, query_adjacent, position, piece[0].shape[0], shard_rows, view_tok)
        for piece, position in zip(pieces, positions)
    ]

    ref = (ref_all[:, :width], ref_all[:, width:])
    key_pieces = [piece[0] for piece in pieces]
    value_pieces = [piece[1] for piece in pieces]
    if view_count == 4:
        state = attention(queries, key_pieces[:2], value_pieces[:2], biases[:2], None, None, 2)
        mixed = attention(queries, key_pieces[2:], value_pieces[2:], biases[2:], state, ref, 2)
    else:
        mixed = attention(queries, key_pieces, value_pieces, biases, None, ref, 2)
    return jnp.dot(mixed, out_weight, preferred_element_type=jnp.float32).astype(jnp.bfloat16)


def solution(mesh):
    return jax.shard_map(
        body,
        mesh=mesh,
        in_specs=(
            P(("mesh", "view"), None),
            P(("mesh", "view"), None),
            P(("mesh", "view"), None),
            P(("mesh", "view"), None),
            P(("mesh", "view"), None),
            P(),
            P("mesh", None),
            P(),
        ),
        out_specs=P(("mesh", "view"), None),
        check_vma=False,
    )
```

```python
import functools

import jax
import jax.numpy as jnp
from jax import lax
from jax.experimental import pallas as pl
from jax.experimental.pallas import tpu as pltpu
from jax.sharding import PartitionSpec as P

HEADS = 20
HEAD_DIM = 64
VIEWS = 6
ADJ = 3
SCALE = 0.125
LANES = 128


def tree_broadcast(value, axis, source):
    count = lax.axis_size(axis)
    index = lax.axis_index(axis)
    if count & (count - 1):
        kept = jnp.where(index == source, value, jnp.zeros_like(value))
        return lax.psum(kept, axis)
    distance = 1
    while distance < count:
        pairs = [(i, i ^ distance) for i in range(count)]
        received = lax.ppermute(value, axis, pairs)
        partner_has = ((index ^ distance) // distance) == (source // distance)
        value = jnp.where(partner_has, received, value)
        distance *= 2
    return value


def gather_rows(value, axis):
    count = lax.axis_size(axis)
    if count == 4:
        across = lax.ppermute(value, axis, [(i, i ^ 2) for i in range(count)])
        both = jnp.concatenate([value, across], axis=0)
        near = lax.ppermute(both, axis, [(i, i ^ 1) for i in range(count)])
        return jnp.concatenate([both, near], axis=0)
    return lax.all_gather(value, axis, axis=0, tiled=True)


def attention_kernel(piece_count, pairs, q_ref, *refs):
    key_refs = refs[:piece_count]
    value_refs = refs[piece_count : 2 * piece_count]
    bias_refs = refs[2 * piece_count : 2 * piece_count + 1]
    rk_ref, rv_ref, out_ref = refs[2 * piece_count + 1 :]
    lane = lax.broadcasted_iota(jnp.int32, (1, LANES), 1)
    dims = (((1,), (1,)), ((), ()))
    for pair in range(pairs):
        cols = slice(pair * LANES, (pair + 1) * LANES)
        queries = q_ref[:, cols]
        results = []
        keys = jnp.concatenate([key_refs[p][:, cols] for p in range(piece_count)], axis=0)
        values = jnp.concatenate([value_refs[p][:, cols] for p in range(piece_count)], axis=0)
        bias = bias_refs[0][...]
        for head in range(LANES // HEAD_DIM):
            own = (lane // HEAD_DIM) == head
            q_head = jnp.where(own, queries, jnp.zeros_like(queries))
            scores = (
                lax.dot_general(q_head, keys, dims, preferred_element_type=jnp.float32) * SCALE + bias
            )
            peak = jnp.max(scores, axis=1, keepdims=True)
            weights = jnp.exp(scores - peak)
            total = jnp.sum(weights, axis=1, keepdims=True)
            summed = jnp.dot(weights.astype(jnp.bfloat16), values, preferred_element_type=jnp.float32)
            view_part = summed / total
            ref_scores = (
                lax.dot_general(q_head, rk_ref[:, cols], dims, preferred_element_type=jnp.float32) * SCALE
            )
            ref_peak = jnp.max(ref_scores, axis=1, keepdims=True)
            ref_weights = jnp.exp(ref_scores - ref_peak)
            ref_total = jnp.sum(ref_weights, axis=1, keepdims=True)
            ref_summed = jnp.dot(
                ref_weights.astype(jnp.bfloat16), rv_ref[:, cols], preferred_element_type=jnp.float32
            )
            results.append((own, view_part + ref_summed / ref_total))
        mixed = results[-1][1]
        for own, value in results[:-1]:
            mixed = jnp.where(own, value, mixed)
        out_ref[:, cols] = mixed.astype(out_ref.dtype)


def attention(queries, key_pieces, value_pieces, biases, ref_keys, ref_values, steps):
    rows, width = queries.shape
    span = width // steps
    column = lambda j: (0, j)
    fixed = lambda j: (0, 0)
    in_specs = [pl.BlockSpec((rows, span), column)]
    in_specs += [pl.BlockSpec((piece.shape[0], span), column) for piece in key_pieces]
    in_specs += [pl.BlockSpec((piece.shape[0], span), column) for piece in value_pieces]
    in_specs += [pl.BlockSpec(bias.shape, fixed) for bias in biases]
    in_specs += [pl.BlockSpec((ref_keys.shape[0], span), column)] * 2
    keys = sum(piece.shape[0] for piece in key_pieces) + ref_keys.shape[0]
    return pl.pallas_call(
        functools.partial(attention_kernel, len(key_pieces), span // LANES),
        grid=(steps,),
        in_specs=in_specs,
        out_specs=pl.BlockSpec((rows, span), column),
        out_shape=jax.ShapeDtypeStruct((rows, width), jnp.bfloat16),
        compiler_params=pltpu.CompilerParams(
            dimension_semantics=("arbitrary",), vmem_limit_bytes=48 * 1024 * 1024
        ),
        cost_estimate=pl.CostEstimate(
            flops=8 * rows * keys * width,
            transcendentals=2 * rows * keys * HEADS,
            bytes_accessed=2 * (2 * rows + 2 * keys) * width + 4 * rows * keys,
        ),
    )(queries, *key_pieces, *value_pieces, *biases, ref_keys, ref_values)


def key_bias(query_views, query_adjacent, position, rows, shard_rows, view_tok):
    key_rows = position * shard_rows + jnp.arange(rows, dtype=jnp.int32)
    key_views = key_rows // view_tok
    keep = query_views[:, None] == key_views[None, :]
    for slot in range(ADJ):
        keep = keep | (query_adjacent[:, slot : slot + 1] == key_views[None, :].astype(jnp.float32))
    return jnp.where(keep, 0.0, -jnp.inf).astype(jnp.float32)


def body(queries, keys, values, ref_keys, ref_values, out_weight, adjacency, ref_source):
    shard_rows, width = queries.shape
    view_count = lax.axis_size("view")
    view_index = lax.axis_index("view")
    view_tok = shard_rows * view_count // VIEWS

    if view_count == 4:
        across = lax.ppermute((keys, values), "view", [(i, i ^ 2) for i in range(view_count)])
        near = lax.ppermute((keys, values), "view", [(i, i ^ 1) for i in range(view_count)])
        far = lax.ppermute(across, "view", [(i, i ^ 1) for i in range(view_count)])
        pieces = [(keys, values), near, across, far]
        positions = [view_index, view_index ^ 1, view_index ^ 2, view_index ^ 3]
    else:
        pieces = [lax.all_gather((keys, values), "view", axis=0, tiled=True)]
        positions = [jnp.zeros((), jnp.int32)]

    ref_both = jnp.concatenate([ref_keys, ref_values], axis=1)
    ref_all = gather_rows(tree_broadcast(ref_both, "mesh", ref_source[0]), "view")

    view_ids = jnp.arange(VIEWS, dtype=jnp.int32)
    query_views = (view_index * shard_rows + jnp.arange(shard_rows, dtype=jnp.int32)) // view_tok
    query_onehot = (query_views[:, None] == view_ids[None, :]).astype(jnp.float32)
    query_adjacent = jnp.dot(query_onehot, adjacency.astype(jnp.float32))
    biases = [
        jnp.concatenate(
            [
                key_bias(query_views, query_adjacent, position, piece[0].shape[0], shard_rows, view_tok)
                for piece, position in zip(pieces, positions)
            ],
            axis=1,
        )
    ]

    mixed = attention(
        queries,
        [piece[0] for piece in pieces],
        [piece[1] for piece in pieces],
        biases,
        ref_all[:, :width],
        ref_all[:, width:],
        2,
    )
    return jnp.dot(mixed, out_weight, preferred_element_type=jnp.float32).astype(jnp.bfloat16)


def solution(mesh):
    return jax.shard_map(
        body,
        mesh=mesh,
        in_specs=(
            P(("mesh", "view"), None),
            P(("mesh", "view"), None),
            P(("mesh", "view"), None),
            P(("mesh", "view"), None),
            P(("mesh", "view"), None),
            P(),
            P("mesh", None),
            P(),
        ),
        out_specs=P(("mesh", "view"), None),
        check_vma=False,
    )
```

```python
import functools

import jax
import jax.numpy as jnp
from jax import lax
from jax.experimental import pallas as pl
from jax.experimental.pallas import tpu as pltpu
from jax.sharding import PartitionSpec as P

HEADS = 20
HEAD_DIM = 64
VIEWS = 6
ADJ = 3
SCALE = 0.125
LANES = 128


def tree_broadcast(value, axis, source):
    count = lax.axis_size(axis)
    index = lax.axis_index(axis)
    if count & (count - 1):
        kept = jnp.where(index == source, value, jnp.zeros_like(value))
        return lax.psum(kept, axis)
    distance = 1
    while distance < count:
        pairs = [(i, i ^ distance) for i in range(count)]
        received = lax.ppermute(value, axis, pairs)
        partner_has = ((index ^ distance) // distance) == (source // distance)
        value = jnp.where(partner_has, received, value)
        distance *= 2
    return value


def gather_rows(value, axis):
    count = lax.axis_size(axis)
    if count == 4:
        across = lax.ppermute(value, axis, [(i, i ^ 2) for i in range(count)])
        both = jnp.concatenate([value, across], axis=0)
        near = lax.ppermute(both, axis, [(i, i ^ 1) for i in range(count)])
        return jnp.concatenate([both, near], axis=0)
    return lax.all_gather(value, axis, axis=0, tiled=True)


def attention_kernel(piece_count, pairs, q_ref, *refs):
    key_refs = refs[:piece_count]
    value_refs = refs[piece_count : 2 * piece_count]
    bias_refs = refs[2 * piece_count : 3 * piece_count]
    rk_ref, rv_ref, out_ref = refs[3 * piece_count :]
    lane = lax.broadcasted_iota(jnp.int32, (1, LANES), 1)
    dims = (((1,), (1,)), ((), ()))
    rows = q_ref.shape[0]
    per_pair = LANES // HEAD_DIM
    for pair in range(pairs):
        cols = slice(pair * LANES, (pair + 1) * LANES)
        queries = q_ref[:, cols]
        stacked = jnp.concatenate(
            [jnp.where((lane // HEAD_DIM) == head, queries, jnp.zeros_like(queries)) for head in range(per_pair)],
            axis=0,
        )
        scores = [
            lax.dot_general(stacked, key_refs[p][:, cols], dims, preferred_element_type=jnp.float32) * SCALE
            + jnp.concatenate([bias_refs[p][...]] * per_pair, axis=0)
            for p in range(piece_count)
        ]
        peak = jnp.max(scores[0], axis=1, keepdims=True)
        for p in range(1, piece_count):
            peak = jnp.maximum(peak, jnp.max(scores[p], axis=1, keepdims=True))
        total = None
        summed = None
        for p in range(piece_count):
            weights = jnp.exp(scores[p] - peak)
            part_total = jnp.sum(weights, axis=1, keepdims=True)
            part = jnp.dot(weights.astype(jnp.bfloat16), value_refs[p][:, cols], preferred_element_type=jnp.float32)
            total = part_total if total is None else total + part_total
            summed = part if summed is None else summed + part
        view_part = summed / total
        ref_scores = lax.dot_general(stacked, rk_ref[:, cols], dims, preferred_element_type=jnp.float32) * SCALE
        ref_peak = jnp.max(ref_scores, axis=1, keepdims=True)
        ref_weights = jnp.exp(ref_scores - ref_peak)
        ref_total = jnp.sum(ref_weights, axis=1, keepdims=True)
        ref_summed = jnp.dot(ref_weights.astype(jnp.bfloat16), rv_ref[:, cols], preferred_element_type=jnp.float32)
        both = view_part + ref_summed / ref_total
        mixed = both[(per_pair - 1) * rows :]
        for head in range(per_pair - 1):
            mixed = jnp.where((lane // HEAD_DIM) == head, both[head * rows : (head + 1) * rows], mixed)
        out_ref[:, cols] = mixed.astype(out_ref.dtype)


def attention(queries, key_pieces, value_pieces, biases, ref_keys, ref_values, steps):
    rows, width = queries.shape
    span = width // steps
    column = lambda j: (0, j)
    fixed = lambda j: (0, 0)
    in_specs = [pl.BlockSpec((rows, span), column)]
    in_specs += [pl.BlockSpec((piece.shape[0], span), column) for piece in key_pieces]
    in_specs += [pl.BlockSpec((piece.shape[0], span), column) for piece in value_pieces]
    in_specs += [pl.BlockSpec(bias.shape, fixed) for bias in biases]
    in_specs += [pl.BlockSpec((ref_keys.shape[0], span), column)] * 2
    keys = sum(piece.shape[0] for piece in key_pieces) + ref_keys.shape[0]
    return pl.pallas_call(
        functools.partial(attention_kernel, len(key_pieces), span // LANES),
        grid=(steps,),
        in_specs=in_specs,
        out_specs=pl.BlockSpec((rows, span), column),
        out_shape=jax.ShapeDtypeStruct((rows, width), jnp.bfloat16),
        compiler_params=pltpu.CompilerParams(
            dimension_semantics=("arbitrary",), vmem_limit_bytes=48 * 1024 * 1024
        ),
        cost_estimate=pl.CostEstimate(
            flops=8 * rows * keys * width,
            transcendentals=2 * rows * keys * HEADS,
            bytes_accessed=2 * (2 * rows + 2 * keys) * width + 4 * rows * keys,
        ),
    )(queries, *key_pieces, *value_pieces, *biases, ref_keys, ref_values)


def key_bias(query_views, query_adjacent, position, rows, shard_rows, view_tok):
    key_rows = position * shard_rows + jnp.arange(rows, dtype=jnp.int32)
    key_views = key_rows // view_tok
    keep = query_views[:, None] == key_views[None, :]
    for slot in range(ADJ):
        keep = keep | (query_adjacent[:, slot : slot + 1] == key_views[None, :].astype(jnp.float32))
    return jnp.where(keep, 0.0, -jnp.inf).astype(jnp.float32)


def body(queries, keys, values, ref_keys, ref_values, out_weight, adjacency, ref_source):
    shard_rows, width = queries.shape
    view_count = lax.axis_size("view")
    view_index = lax.axis_index("view")
    view_tok = shard_rows * view_count // VIEWS

    if view_count == 4:
        across = lax.ppermute((keys, values), "view", [(i, i ^ 2) for i in range(view_count)])
        near = lax.ppermute((keys, values), "view", [(i, i ^ 1) for i in range(view_count)])
        far = lax.ppermute(across, "view", [(i, i ^ 1) for i in range(view_count)])
        pieces = [(keys, values), near, across, far]
        positions = [view_index, view_index ^ 1, view_index ^ 2, view_index ^ 3]
    else:
        pieces = [lax.all_gather((keys, values), "view", axis=0, tiled=True)]
        positions = [jnp.zeros((), jnp.int32)]

    ref_both = jnp.concatenate([ref_keys, ref_values], axis=1)
    ref_all = gather_rows(tree_broadcast(ref_both, "mesh", ref_source[0]), "view")

    view_ids = jnp.arange(VIEWS, dtype=jnp.int32)
    query_views = (view_index * shard_rows + jnp.arange(shard_rows, dtype=jnp.int32)) // view_tok
    query_onehot = (query_views[:, None] == view_ids[None, :]).astype(jnp.float32)
    query_adjacent = jnp.dot(query_onehot, adjacency.astype(jnp.float32))
    biases = [
        key_bias(query_views, query_adjacent, position, piece[0].shape[0], shard_rows, view_tok)
        for piece, position in zip(pieces, positions)
    ]

    mixed = attention(
        queries,
        [piece[0] for piece in pieces],
        [piece[1] for piece in pieces],
        biases,
        ref_all[:, :width],
        ref_all[:, width:],
        1,
    )
    return jnp.dot(mixed, out_weight, preferred_element_type=jnp.float32).astype(jnp.bfloat16)


def solution(mesh):
    return jax.shard_map(
        body,
        mesh=mesh,
        in_specs=(
            P(("mesh", "view"), None),
            P(("mesh", "view"), None),
            P(("mesh", "view"), None),
            P(("mesh", "view"), None),
            P(("mesh", "view"), None),
            P(),
            P("mesh", None),
            P(),
        ),
        out_specs=P(("mesh", "view"), None),
        check_vma=False,
    )
```

```python
import functools

import jax
import jax.numpy as jnp
from jax import lax
from jax.experimental import pallas as pl
from jax.experimental.pallas import tpu as pltpu
from jax.sharding import PartitionSpec as P

HEADS = 20
HEAD_DIM = 64
VIEWS = 6
ADJ = 3
SCALE = 0.125
LANES = 128


def tree_broadcast(value, axis, source):
    count = lax.axis_size(axis)
    index = lax.axis_index(axis)
    if count & (count - 1):
        kept = jnp.where(index == source, value, jnp.zeros_like(value))
        return lax.psum(kept, axis)
    distance = 1
    while distance < count:
        pairs = [(i, i ^ distance) for i in range(count)]
        received = lax.ppermute(value, axis, pairs)
        partner_has = ((index ^ distance) // distance) == (source // distance)
        value = jnp.where(partner_has, received, value)
        distance *= 2
    return value


def gather_rows(value, axis):
    count = lax.axis_size(axis)
    if count == 4:
        across = lax.ppermute(value, axis, [(i, i ^ 2) for i in range(count)])
        both = jnp.concatenate([value, across], axis=0)
        near = lax.ppermute(both, axis, [(i, i ^ 1) for i in range(count)])
        return jnp.concatenate([both, near], axis=0)
    return lax.all_gather(value, axis, axis=0, tiled=True)


def attention_kernel(piece_count, ref_count, pairs, q_ref, *refs):
    key_refs = refs[:piece_count]
    value_refs = refs[piece_count : 2 * piece_count]
    bias_refs = refs[2 * piece_count : 3 * piece_count]
    rk_refs = refs[3 * piece_count : 3 * piece_count + ref_count]
    rv_refs = refs[3 * piece_count + ref_count : 3 * piece_count + 2 * ref_count]
    out_ref = refs[-1]
    lane = lax.broadcasted_iota(jnp.int32, (1, LANES), 1)
    dims = (((1,), (1,)), ((), ()))
    rows = q_ref.shape[0]
    per_pair = LANES // HEAD_DIM
    for pair in range(pairs):
        cols = slice(pair * LANES, (pair + 1) * LANES)
        queries = q_ref[:, cols]
        stacked = jnp.concatenate(
            [jnp.where((lane // HEAD_DIM) == head, queries, jnp.zeros_like(queries)) for head in range(per_pair)],
            axis=0,
        )
        scores = [
            lax.dot_general(stacked, key_refs[p][:, cols], dims, preferred_element_type=jnp.float32) * SCALE
            + bias_refs[p][...]
            for p in range(piece_count)
        ]
        peak = jnp.max(scores[0], axis=1, keepdims=True)
        for p in range(1, piece_count):
            peak = jnp.maximum(peak, jnp.max(scores[p], axis=1, keepdims=True))
        total = None
        summed = None
        for p in range(piece_count):
            weights = jnp.exp(scores[p] - peak)
            part_total = jnp.sum(weights, axis=1, keepdims=True)
            part = jnp.dot(weights.astype(jnp.bfloat16), value_refs[p][:, cols], preferred_element_type=jnp.float32)
            total = part_total if total is None else total + part_total
            summed = part if summed is None else summed + part
        view_part = summed / total
        ref_keys = jnp.concatenate([r[:, cols] for r in rk_refs], axis=0)
        ref_values = jnp.concatenate([r[:, cols] for r in rv_refs], axis=0)
        ref_scores = lax.dot_general(stacked, ref_keys, dims, preferred_element_type=jnp.float32) * SCALE
        ref_peak = jnp.max(ref_scores, axis=1, keepdims=True)
        ref_weights = jnp.exp(ref_scores - ref_peak)
        ref_total = jnp.sum(ref_weights, axis=1, keepdims=True)
        ref_summed = jnp.dot(ref_weights.astype(jnp.bfloat16), ref_values, preferred_element_type=jnp.float32)
        both = view_part + ref_summed / ref_total
        mixed = both[(per_pair - 1) * rows :]
        for head in range(per_pair - 1):
            mixed = jnp.where((lane // HEAD_DIM) == head, both[head * rows : (head + 1) * rows], mixed)
        out_ref[:, cols] = mixed.astype(out_ref.dtype)


def attention(queries, key_pieces, value_pieces, biases, ref_pieces, steps):
    rows, width = queries.shape
    span = width // steps
    column = lambda j: (0, j)
    second = lambda j: (0, j + steps)
    fixed = lambda j: (0, 0)
    in_specs = [pl.BlockSpec((rows, span), column)]
    in_specs += [pl.BlockSpec((piece.shape[0], span), column) for piece in key_pieces]
    in_specs += [pl.BlockSpec((piece.shape[0], span), column) for piece in value_pieces]
    in_specs += [pl.BlockSpec(bias.shape, fixed) for bias in biases]
    in_specs += [pl.BlockSpec((piece.shape[0], span), column) for piece in ref_pieces]
    in_specs += [pl.BlockSpec((piece.shape[0], span), second) for piece in ref_pieces]
    keys = sum(piece.shape[0] for piece in key_pieces) + sum(piece.shape[0] for piece in ref_pieces)
    return pl.pallas_call(
        functools.partial(attention_kernel, len(key_pieces), len(ref_pieces), span // LANES),
        grid=(steps,),
        in_specs=in_specs,
        out_specs=pl.BlockSpec((rows, span), column),
        out_shape=jax.ShapeDtypeStruct((rows, width), jnp.bfloat16),
        compiler_params=pltpu.CompilerParams(
            dimension_semantics=("arbitrary",), vmem_limit_bytes=64 * 1024 * 1024
        ),
        cost_estimate=pl.CostEstimate(
            flops=8 * rows * keys * width,
            transcendentals=2 * rows * keys * HEADS,
            bytes_accessed=2 * (2 * rows + 2 * keys) * width + 8 * rows * keys,
        ),
    )(queries, *key_pieces, *value_pieces, *biases, *ref_pieces, *ref_pieces)


def key_bias(query_views, query_adjacent, position, rows, shard_rows, view_tok):
    key_rows = position * shard_rows + jnp.arange(rows, dtype=jnp.int32)
    key_views = key_rows // view_tok
    keep = query_views[:, None] == key_views[None, :]
    for slot in range(ADJ):
        keep = keep | (query_adjacent[:, slot : slot + 1] == key_views[None, :].astype(jnp.float32))
    return jnp.where(keep, 0.0, -jnp.inf).astype(jnp.float32)


def body(queries, keys, values, ref_keys, ref_values, out_weight, adjacency, ref_source):
    shard_rows, width = queries.shape
    view_count = lax.axis_size("view")
    view_index = lax.axis_index("view")
    view_tok = shard_rows * view_count // VIEWS

    ref_both = jnp.concatenate([ref_keys, ref_values], axis=1)
    ref_shared = tree_broadcast(ref_both, "mesh", ref_source[0])
    if view_count == 4:
        across = lax.ppermute((keys, values), "view", [(i, i ^ 2) for i in range(view_count)])
        near = lax.ppermute((keys, values), "view", [(i, i ^ 1) for i in range(view_count)])
        ref_shared, across = lax.optimization_barrier((ref_shared, across))
        far = lax.ppermute(across, "view", [(i, i ^ 1) for i in range(view_count)])
        ref_across = lax.ppermute(ref_shared, "view", [(i, i ^ 2) for i in range(view_count)])
        ref_near = lax.ppermute((ref_shared, ref_across), "view", [(i, i ^ 1) for i in range(view_count)])
        pieces = [(keys, values), near, across, far]
        positions = [view_index, view_index ^ 1, view_index ^ 2, view_index ^ 3]
        ref_pieces = [ref_shared, ref_across, *ref_near]
    else:
        pieces = [lax.all_gather((keys, values), "view", axis=0, tiled=True)]
        positions = [jnp.zeros((), jnp.int32)]
        ref_pieces = [lax.all_gather(ref_shared, "view", axis=0, tiled=True)]

    view_ids = jnp.arange(VIEWS, dtype=jnp.int32)
    query_views = (view_index * shard_rows + jnp.arange(shard_rows, dtype=jnp.int32)) // view_tok
    query_onehot = (query_views[:, None] == view_ids[None, :]).astype(jnp.float32)
    query_adjacent = jnp.dot(query_onehot, adjacency.astype(jnp.float32))
    biases = [
        jnp.concatenate(
            [key_bias(query_views, query_adjacent, position, piece[0].shape[0], shard_rows, view_tok)] * 2, axis=0
        )
        for piece, position in zip(pieces, positions)
    ]
    mixed = attention(
        queries, [piece[0] for piece in pieces], [piece[1] for piece in pieces], biases, ref_pieces, 1 if view_count == 4 else 2
    )
    return jnp.dot(mixed, out_weight, preferred_element_type=jnp.float32).astype(jnp.bfloat16)


def solution(mesh):
    return jax.shard_map(
        body,
        mesh=mesh,
        in_specs=(
            P(("mesh", "view"), None),
            P(("mesh", "view"), None),
            P(("mesh", "view"), None),
            P(("mesh", "view"), None),
            P(("mesh", "view"), None),
            P(),
            P("mesh", None),
            P(),
        ),
        out_specs=P(("mesh", "view"), None),
        check_vma=False,
    )
```

```python
import functools

import jax
import jax.numpy as jnp
from jax import lax
from jax.experimental import pallas as pl
from jax.experimental.pallas import tpu as pltpu
from jax.sharding import PartitionSpec as P

HEADS = 20
HEAD_DIM = 64
VIEWS = 6
ADJ = 3
SCALE = 0.125
LANES = 128


def tree_broadcast(value, axis, source):
    count = lax.axis_size(axis)
    index = lax.axis_index(axis)
    if count & (count - 1):
        kept = jnp.where(index == source, value, jnp.zeros_like(value))
        return lax.psum(kept, axis)
    distance = 1
    while distance < count:
        pairs = [(i, i ^ distance) for i in range(count)]
        received = lax.ppermute(value, axis, pairs)
        partner_has = ((index ^ distance) // distance) == (source // distance)
        value = jnp.where(partner_has, received, value)
        distance *= 2
    return value


def gather_rows(value, axis):
    count = lax.axis_size(axis)
    if count == 4:
        across = lax.ppermute(value, axis, [(i, i ^ 2) for i in range(count)])
        both = jnp.concatenate([value, across], axis=0)
        near = lax.ppermute(both, axis, [(i, i ^ 1) for i in range(count)])
        return jnp.concatenate([both, near], axis=0)
    return lax.all_gather(value, axis, axis=0, tiled=True)


def attention_kernel(piece_count, pairs, q_ref, *refs):
    key_refs = refs[:piece_count]
    value_refs = refs[piece_count : 2 * piece_count]
    bias_refs = refs[2 * piece_count : 3 * piece_count]
    rk_ref, rv_ref, out_ref = refs[3 * piece_count :]
    lane = lax.broadcasted_iota(jnp.int32, (1, LANES), 1)
    dims = (((1,), (1,)), ((), ()))
    rows = q_ref.shape[0]
    per_pair = LANES // HEAD_DIM
    for pair in range(pairs):
        cols = slice(pair * LANES, (pair + 1) * LANES)
        queries = q_ref[:, cols]
        stacked = jnp.concatenate(
            [jnp.where((lane // HEAD_DIM) == head, queries, jnp.zeros_like(queries)) for head in range(per_pair)],
            axis=0,
        )
        scores = [
            lax.dot_general(stacked, key_refs[p][:, cols], dims, preferred_element_type=jnp.float32) * SCALE
            + jnp.concatenate([bias_refs[p][...]] * per_pair, axis=0)
            for p in range(piece_count)
        ]
        peak = jnp.max(scores[0], axis=1, keepdims=True)
        for p in range(1, piece_count):
            peak = jnp.maximum(peak, jnp.max(scores[p], axis=1, keepdims=True))
        total = None
        summed = None
        for p in range(piece_count):
            weights = jnp.exp(scores[p] - peak)
            part_total = jnp.sum(weights, axis=1, keepdims=True)
            part = jnp.dot(weights.astype(jnp.bfloat16), value_refs[p][:, cols], preferred_element_type=jnp.float32)
            total = part_total if total is None else total + part_total
            summed = part if summed is None else summed + part
        view_part = summed / total
        ref_scores = lax.dot_general(stacked, rk_ref[:, cols], dims, preferred_element_type=jnp.float32) * SCALE
        ref_peak = jnp.max(ref_scores, axis=1, keepdims=True)
        ref_weights = jnp.exp(ref_scores - ref_peak)
        ref_total = jnp.sum(ref_weights, axis=1, keepdims=True)
        ref_summed = jnp.dot(ref_weights.astype(jnp.bfloat16), rv_ref[:, cols], preferred_element_type=jnp.float32)
        both = view_part + ref_summed / ref_total
        mixed = both[(per_pair - 1) * rows :]
        for head in range(per_pair - 1):
            mixed = jnp.where((lane // HEAD_DIM) == head, both[head * rows : (head + 1) * rows], mixed)
        out_ref[:, cols] = mixed.astype(out_ref.dtype)


def attention(queries, key_pieces, value_pieces, biases, ref_keys, ref_values, steps):
    rows, width = queries.shape
    span = width // steps
    column = lambda j: (0, j)
    fixed = lambda j: (0, 0)
    in_specs = [pl.BlockSpec((rows, span), column)]
    in_specs += [pl.BlockSpec((piece.shape[0], span), column) for piece in key_pieces]
    in_specs += [pl.BlockSpec((piece.shape[0], span), column) for piece in value_pieces]
    in_specs += [pl.BlockSpec(bias.shape, fixed) for bias in biases]
    in_specs += [pl.BlockSpec((ref_keys.shape[0], span), column)] * 2
    keys = sum(piece.shape[0] for piece in key_pieces) + ref_keys.shape[0]
    return pl.pallas_call(
        functools.partial(attention_kernel, len(key_pieces), span // LANES),
        grid=(steps,),
        in_specs=in_specs,
        out_specs=pl.BlockSpec((rows, span), column),
        out_shape=jax.ShapeDtypeStruct((rows, width), jnp.bfloat16),
        compiler_params=pltpu.CompilerParams(
            dimension_semantics=("arbitrary",), vmem_limit_bytes=48 * 1024 * 1024
        ),
        cost_estimate=pl.CostEstimate(
            flops=8 * rows * keys * width,
            transcendentals=2 * rows * keys * HEADS,
            bytes_accessed=2 * (2 * rows + 2 * keys) * width + 4 * rows * keys,
        ),
    )(queries, *key_pieces, *value_pieces, *biases, ref_keys, ref_values)


def key_bias(query_views, query_adjacent, position, rows, shard_rows, view_tok):
    key_rows = position * shard_rows + jnp.arange(rows, dtype=jnp.int32)
    key_views = key_rows // view_tok
    keep = query_views[:, None] == key_views[None, :]
    for slot in range(ADJ):
        keep = keep | (query_adjacent[:, slot : slot + 1] == key_views[None, :].astype(jnp.float32))
    return jnp.where(keep, 0.0, -jnp.inf).astype(jnp.float32)


def body(queries, keys, values, ref_keys, ref_values, out_weight, adjacency, ref_source):
    shard_rows, width = queries.shape
    view_count = lax.axis_size("view")
    view_index = lax.axis_index("view")
    view_tok = shard_rows * view_count // VIEWS

    ref_both = jnp.concatenate([ref_keys, ref_values], axis=1)
    ref_shared = tree_broadcast(ref_both, "mesh", ref_source[0])
    if view_count == 4:
        across = lax.ppermute((keys, values), "view", [(i, i ^ 2) for i in range(view_count)])
        near = lax.ppermute((keys, values), "view", [(i, i ^ 1) for i in range(view_count)])
        ref_shared, across = lax.optimization_barrier((ref_shared, across))
        far = lax.ppermute(across, "view", [(i, i ^ 1) for i in range(view_count)])
        pieces = [(keys, values), near, across, far]
        positions = [view_index, view_index ^ 1, view_index ^ 2, view_index ^ 3]
    else:
        pieces = [lax.all_gather((keys, values), "view", axis=0, tiled=True)]
        positions = [jnp.zeros((), jnp.int32)]
    ref_all = gather_rows(ref_shared, "view")

    view_ids = jnp.arange(VIEWS, dtype=jnp.int32)
    query_views = (view_index * shard_rows + jnp.arange(shard_rows, dtype=jnp.int32)) // view_tok
    query_onehot = (query_views[:, None] == view_ids[None, :]).astype(jnp.float32)
    query_adjacent = jnp.dot(query_onehot, adjacency.astype(jnp.float32))
    biases = [
        key_bias(query_views, query_adjacent, position, piece[0].shape[0], shard_rows, view_tok)
        for piece, position in zip(pieces, positions)
    ]

    mixed = attention(
        queries,
        [piece[0] for piece in pieces],
        [piece[1] for piece in pieces],
        biases,
        ref_all[:, :width],
        ref_all[:, width:],
        1,
    )
    return jnp.dot(mixed, out_weight, preferred_element_type=jnp.float32).astype(jnp.bfloat16)


def solution(mesh):
    return jax.shard_map(
        body,
        mesh=mesh,
        in_specs=(
            P(("mesh", "view"), None),
            P(("mesh", "view"), None),
            P(("mesh", "view"), None),
            P(("mesh", "view"), None),
            P(("mesh", "view"), None),
            P(),
            P("mesh", None),
            P(),
        ),
        out_specs=P(("mesh", "view"), None),
        check_vma=False,
    )
```

```python
import functools

import jax
import jax.numpy as jnp
from jax import lax
from jax.experimental import pallas as pl
from jax.experimental.pallas import tpu as pltpu
from jax.sharding import PartitionSpec as P

HEADS = 20
HEAD_DIM = 64
VIEWS = 6
ADJ = 3
SCALE = 0.125
LANES = 128


def tree_broadcast(value, axis, source):
    count = lax.axis_size(axis)
    index = lax.axis_index(axis)
    if count & (count - 1):
        kept = jnp.where(index == source, value, jnp.zeros_like(value))
        return lax.psum(kept, axis)
    distance = count // 2
    while distance >= 1:
        pairs = [(i, i ^ distance) for i in range(count)]
        received = lax.ppermute(value, axis, pairs)
        partner_has = ((index ^ distance) % (2 * distance)) == (source % (2 * distance))
        value = jnp.where(partner_has, received, value)
        distance //= 2
    return value


def gather_rows(value, axis):
    count = lax.axis_size(axis)
    if count == 4:
        across = lax.ppermute(value, axis, [(i, i ^ 2) for i in range(count)])
        both = jnp.concatenate([value, across], axis=0)
        near = lax.ppermute(both, axis, [(i, i ^ 1) for i in range(count)])
        return jnp.concatenate([both, near], axis=0)
    return lax.all_gather(value, axis, axis=0, tiled=True)


def attention_kernel(piece_count, pairs, q_ref, *refs):
    key_refs = refs[:piece_count]
    value_refs = refs[piece_count : 2 * piece_count]
    bias_refs = refs[2 * piece_count : 3 * piece_count]
    rk_ref, rv_ref, out_ref = refs[3 * piece_count :]
    lane = lax.broadcasted_iota(jnp.int32, (1, LANES), 1)
    dims = (((1,), (1,)), ((), ()))
    rows = q_ref.shape[0]
    per_pair = LANES // HEAD_DIM
    for pair in range(pairs):
        cols = slice(pair * LANES, (pair + 1) * LANES)
        queries = q_ref[:, cols]
        stacked = jnp.concatenate(
            [jnp.where((lane // HEAD_DIM) == head, queries, jnp.zeros_like(queries)) for head in range(per_pair)],
            axis=0,
        )
        scores = [
            lax.dot_general(stacked, key_refs[p][:, cols], dims, preferred_element_type=jnp.float32) * SCALE
            + jnp.concatenate([bias_refs[p][...]] * per_pair, axis=0)
            for p in range(piece_count)
        ]
        peak = jnp.max(scores[0], axis=1, keepdims=True)
        for p in range(1, piece_count):
            peak = jnp.maximum(peak, jnp.max(scores[p], axis=1, keepdims=True))
        total = None
        summed = None
        for p in range(piece_count):
            weights = jnp.exp(scores[p] - peak)
            part_total = jnp.sum(weights, axis=1, keepdims=True)
            part = jnp.dot(weights.astype(jnp.bfloat16), value_refs[p][:, cols], preferred_element_type=jnp.float32)
            total = part_total if total is None else total + part_total
            summed = part if summed is None else summed + part
        view_part = summed / total
        ref_scores = lax.dot_general(stacked, rk_ref[:, cols], dims, preferred_element_type=jnp.float32) * SCALE
        ref_peak = jnp.max(ref_scores, axis=1, keepdims=True)
        ref_weights = jnp.exp(ref_scores - ref_peak)
        ref_total = jnp.sum(ref_weights, axis=1, keepdims=True)
        ref_summed = jnp.dot(ref_weights.astype(jnp.bfloat16), rv_ref[:, cols], preferred_element_type=jnp.float32)
        both = view_part + ref_summed / ref_total
        mixed = both[(per_pair - 1) * rows :]
        for head in range(per_pair - 1):
            mixed = jnp.where((lane // HEAD_DIM) == head, both[head * rows : (head + 1) * rows], mixed)
        out_ref[:, cols] = mixed.astype(out_ref.dtype)


def attention(queries, key_pieces, value_pieces, biases, ref_keys, ref_values, steps):
    rows, width = queries.shape
    span = width // steps
    column = lambda j: (0, j)
    fixed = lambda j: (0, 0)
    in_specs = [pl.BlockSpec((rows, span), column)]
    in_specs += [pl.BlockSpec((piece.shape[0], span), column) for piece in key_pieces]
    in_specs += [pl.BlockSpec((piece.shape[0], span), column) for piece in value_pieces]
    in_specs += [pl.BlockSpec(bias.shape, fixed) for bias in biases]
    in_specs += [pl.BlockSpec((ref_keys.shape[0], span), column)] * 2
    keys = sum(piece.shape[0] for piece in key_pieces) + ref_keys.shape[0]
    return pl.pallas_call(
        functools.partial(attention_kernel, len(key_pieces), span // LANES),
        grid=(steps,),
        in_specs=in_specs,
        out_specs=pl.BlockSpec((rows, span), column),
        out_shape=jax.ShapeDtypeStruct((rows, width), jnp.bfloat16),
        compiler_params=pltpu.CompilerParams(
            dimension_semantics=("arbitrary",), vmem_limit_bytes=48 * 1024 * 1024
        ),
        cost_estimate=pl.CostEstimate(
            flops=8 * rows * keys * width,
            transcendentals=2 * rows * keys * HEADS,
            bytes_accessed=2 * (2 * rows + 2 * keys) * width + 4 * rows * keys,
        ),
    )(queries, *key_pieces, *value_pieces, *biases, ref_keys, ref_values)


def key_bias(query_views, query_adjacent, position, rows, shard_rows, view_tok):
    key_rows = position * shard_rows + jnp.arange(rows, dtype=jnp.int32)
    key_views = key_rows // view_tok
    keep = query_views[:, None] == key_views[None, :]
    for slot in range(ADJ):
        keep = keep | (query_adjacent[:, slot : slot + 1] == key_views[None, :].astype(jnp.float32))
    return jnp.where(keep, 0.0, -jnp.inf).astype(jnp.float32)


def body(queries, keys, values, ref_keys, ref_values, out_weight, adjacency, ref_source):
    shard_rows, width = queries.shape
    view_count = lax.axis_size("view")
    view_index = lax.axis_index("view")
    view_tok = shard_rows * view_count // VIEWS

    ref_both = jnp.concatenate([ref_keys, ref_values], axis=1)
    ref_shared = tree_broadcast(ref_both, "mesh", ref_source[0])
    if view_count == 4:
        across = lax.ppermute((keys, values), "view", [(i, i ^ 2) for i in range(view_count)])
        near = lax.ppermute((keys, values), "view", [(i, i ^ 1) for i in range(view_count)])
        ref_shared, across = lax.optimization_barrier((ref_shared, across))
        far = lax.ppermute(across, "view", [(i, i ^ 1) for i in range(view_count)])
        pieces = [(keys, values), near, across, far]
        positions = [view_index, view_index ^ 1, view_index ^ 2, view_index ^ 3]
    else:
        pieces = [lax.all_gather((keys, values), "view", axis=0, tiled=True)]
        positions = [jnp.zeros((), jnp.int32)]
    ref_all = gather_rows(ref_shared, "view")

    view_ids = jnp.arange(VIEWS, dtype=jnp.int32)
    query_views = (view_index * shard_rows + jnp.arange(shard_rows, dtype=jnp.int32)) // view_tok
    query_onehot = (query_views[:, None] == view_ids[None, :]).astype(jnp.float32)
    query_adjacent = jnp.dot(query_onehot, adjacency.astype(jnp.float32))
    biases = [
        key_bias(query_views, query_adjacent, position, piece[0].shape[0], shard_rows, view_tok)
        for piece, position in zip(pieces, positions)
    ]

    mixed = attention(
        queries,
        [piece[0] for piece in pieces],
        [piece[1] for piece in pieces],
        biases,
        ref_all[:, :width],
        ref_all[:, width:],
        1,
    )
    return jnp.dot(mixed, out_weight, preferred_element_type=jnp.float32).astype(jnp.bfloat16)


def solution(mesh):
    return jax.shard_map(
        body,
        mesh=mesh,
        in_specs=(
            P(("mesh", "view"), None),
            P(("mesh", "view"), None),
            P(("mesh", "view"), None),
            P(("mesh", "view"), None),
            P(("mesh", "view"), None),
            P(),
            P("mesh", None),
            P(),
        ),
        out_specs=P(("mesh", "view"), None),
        check_vma=False,
    )
```

```python
import functools

import jax
import jax.numpy as jnp
from jax import lax
from jax.experimental import pallas as pl
from jax.experimental.pallas import tpu as pltpu
from jax.sharding import PartitionSpec as P

HEADS = 20
HEAD_DIM = 64
VIEWS = 6
ADJ = 3
SCALE = 0.125
LANES = 128


def tree_broadcast(value, axis, source):
    count = lax.axis_size(axis)
    index = lax.axis_index(axis)
    if count & (count - 1):
        kept = jnp.where(index == source, value, jnp.zeros_like(value))
        return lax.psum(kept, axis)
    distance = 1
    while distance < count:
        pairs = [(i, i ^ distance) for i in range(count)]
        received = lax.ppermute(value, axis, pairs)
        partner_has = ((index ^ distance) // distance) == (source // distance)
        value = jnp.where(partner_has, received, value)
        distance *= 2
    return value


def gather_rows(value, axis):
    count = lax.axis_size(axis)
    if count == 4:
        across = lax.ppermute(value, axis, [(i, i ^ 2) for i in range(count)])
        both = jnp.concatenate([value, across], axis=0)
        near = lax.ppermute(both, axis, [(i, i ^ 1) for i in range(count)])
        return jnp.concatenate([both, near], axis=0)
    return lax.all_gather(value, axis, axis=0, tiled=True)


def attention_kernel(piece_count, pairs, q_ref, *refs):
    key_refs = refs[:piece_count]
    value_refs = refs[piece_count : 2 * piece_count]
    bias_refs = refs[2 * piece_count : 3 * piece_count]
    rk_ref, rv_ref, out_ref = refs[3 * piece_count :]
    lane = lax.broadcasted_iota(jnp.int32, (1, LANES), 1)
    dims = (((1,), (1,)), ((), ()))
    rows = q_ref.shape[0]
    per_pair = LANES // HEAD_DIM
    for pair in range(pairs):
        cols = slice(pair * LANES, (pair + 1) * LANES)
        queries = q_ref[:, cols]
        stacked = jnp.concatenate(
            [jnp.where((lane // HEAD_DIM) == head, queries, jnp.zeros_like(queries)) for head in range(per_pair)],
            axis=0,
        )
        scores = [
            lax.dot_general(stacked, key_refs[p][:, cols], dims, preferred_element_type=jnp.float32) * SCALE
            + jnp.concatenate([bias_refs[p][...]] * per_pair, axis=0)
            for p in range(piece_count)
        ]
        peak = jnp.max(scores[0], axis=1, keepdims=True)
        for p in range(1, piece_count):
            peak = jnp.maximum(peak, jnp.max(scores[p], axis=1, keepdims=True))
        total = None
        summed = None
        for p in range(piece_count):
            weights = jnp.exp(scores[p] - peak)
            part_total = jnp.sum(weights, axis=1, keepdims=True)
            part = jnp.dot(weights.astype(jnp.bfloat16), value_refs[p][:, cols], preferred_element_type=jnp.float32)
            total = part_total if total is None else total + part_total
            summed = part if summed is None else summed + part
        view_part = summed / total
        ref_scores = lax.dot_general(stacked, rk_ref[:, cols], dims, preferred_element_type=jnp.float32) * SCALE
        ref_peak = jnp.max(ref_scores, axis=1, keepdims=True)
        ref_weights = jnp.exp(ref_scores - ref_peak)
        ref_total = jnp.sum(ref_weights, axis=1, keepdims=True)
        ref_summed = jnp.dot(ref_weights.astype(jnp.bfloat16), rv_ref[:, cols], preferred_element_type=jnp.float32)
        both = view_part + ref_summed / ref_total
        mixed = both[(per_pair - 1) * rows :]
        for head in range(per_pair - 1):
            mixed = jnp.where((lane // HEAD_DIM) == head, both[head * rows : (head + 1) * rows], mixed)
        out_ref[:, cols] = mixed.astype(out_ref.dtype)


def attention(queries, key_pieces, value_pieces, biases, ref_keys, ref_values, steps):
    rows, width = queries.shape
    span = width // steps
    column = lambda j: (0, j)
    fixed = lambda j: (0, 0)
    in_specs = [pl.BlockSpec((rows, span), column)]
    in_specs += [pl.BlockSpec((piece.shape[0], span), column) for piece in key_pieces]
    in_specs += [pl.BlockSpec((piece.shape[0], span), column) for piece in value_pieces]
    in_specs += [pl.BlockSpec(bias.shape, fixed) for bias in biases]
    in_specs += [pl.BlockSpec((ref_keys.shape[0], span), column)] * 2
    keys = sum(piece.shape[0] for piece in key_pieces) + ref_keys.shape[0]
    return pl.pallas_call(
        functools.partial(attention_kernel, len(key_pieces), span // LANES),
        grid=(steps,),
        in_specs=in_specs,
        out_specs=pl.BlockSpec((rows, span), column),
        out_shape=jax.ShapeDtypeStruct((rows, width), jnp.bfloat16),
        compiler_params=pltpu.CompilerParams(
            dimension_semantics=("arbitrary",), vmem_limit_bytes=48 * 1024 * 1024
        ),
        cost_estimate=pl.CostEstimate(
            flops=8 * rows * keys * width,
            transcendentals=2 * rows * keys * HEADS,
            bytes_accessed=2 * (2 * rows + 2 * keys) * width + 4 * rows * keys,
        ),
    )(queries, *key_pieces, *value_pieces, *biases, ref_keys, ref_values)


def key_bias(query_views, query_adjacent, position, rows, shard_rows, view_tok):
    key_rows = position * shard_rows + jnp.arange(rows, dtype=jnp.int32)
    key_views = key_rows // view_tok
    keep = query_views[:, None] == key_views[None, :]
    for slot in range(ADJ):
        keep = keep | (query_adjacent[:, slot : slot + 1] == key_views[None, :].astype(jnp.float32))
    return jnp.where(keep, 0.0, -jnp.inf).astype(jnp.float32)


def body(queries, keys, values, ref_keys, ref_values, out_weight, adjacency, ref_source):
    shard_rows, width = queries.shape
    view_count = lax.axis_size("view")
    view_index = lax.axis_index("view")
    view_tok = shard_rows * view_count // VIEWS

    ref_both = jnp.concatenate([ref_keys, ref_values], axis=0)
    ref_shared = tree_broadcast(ref_both, "mesh", ref_source[0])
    if view_count == 4:
        across = lax.ppermute((keys, values), "view", [(i, i ^ 2) for i in range(view_count)])
        near = lax.ppermute((keys, values), "view", [(i, i ^ 1) for i in range(view_count)])
        ref_shared, across = lax.optimization_barrier((ref_shared, across))
        far = lax.ppermute(across, "view", [(i, i ^ 1) for i in range(view_count)])
        pieces = [(keys, values), near, across, far]
        positions = [view_index, view_index ^ 1, view_index ^ 2, view_index ^ 3]
    else:
        pieces = [lax.all_gather((keys, values), "view", axis=0, tiled=True)]
        positions = [jnp.zeros((), jnp.int32)]
    ref_all = gather_rows(ref_shared, "view")
    ref_blocks = ref_all.reshape(-1, 2, ref_keys.shape[0], width)
    ref_key_rows = ref_blocks[:, 0].reshape(-1, width)
    ref_value_rows = ref_blocks[:, 1].reshape(-1, width)

    view_ids = jnp.arange(VIEWS, dtype=jnp.int32)
    query_views = (view_index * shard_rows + jnp.arange(shard_rows, dtype=jnp.int32)) // view_tok
    query_onehot = (query_views[:, None] == view_ids[None, :]).astype(jnp.float32)
    query_adjacent = jnp.dot(query_onehot, adjacency.astype(jnp.float32))
    biases = [
        key_bias(query_views, query_adjacent, position, piece[0].shape[0], shard_rows, view_tok)
        for piece, position in zip(pieces, positions)
    ]

    mixed = attention(
        queries,
        [piece[0] for piece in pieces],
        [piece[1] for piece in pieces],
        biases,
        ref_key_rows,
        ref_value_rows,
        1,
    )
    return jnp.dot(mixed, out_weight, preferred_element_type=jnp.float32).astype(jnp.bfloat16)


def solution(mesh):
    return jax.shard_map(
        body,
        mesh=mesh,
        in_specs=(
            P(("mesh", "view"), None),
            P(("mesh", "view"), None),
            P(("mesh", "view"), None),
            P(("mesh", "view"), None),
            P(("mesh", "view"), None),
            P(),
            P("mesh", None),
            P(),
        ),
        out_specs=P(("mesh", "view"), None),
        check_vma=False,
    )
```

```python
import functools

import jax
import jax.numpy as jnp
from jax import lax
from jax.experimental import pallas as pl
from jax.experimental.pallas import tpu as pltpu
from jax.sharding import PartitionSpec as P

HEADS = 20
HEAD_DIM = 64
VIEWS = 6
ADJ = 3
SCALE = 0.125
LANES = 128


def tree_broadcast(value, axis, source):
    count = lax.axis_size(axis)
    index = lax.axis_index(axis)
    if count & (count - 1):
        kept = jnp.where(index == source, value, jnp.zeros_like(value))
        return lax.psum(kept, axis)
    distance = 1
    while distance < count:
        pairs = [(i, i ^ distance) for i in range(count)]
        received = lax.ppermute(value, axis, pairs)
        partner_has = ((index ^ distance) // distance) == (source // distance)
        value = jnp.where(partner_has, received, value)
        distance *= 2
    return value


def gather_rows(value, axis):
    count = lax.axis_size(axis)
    if count == 4:
        across = lax.ppermute(value, axis, [(i, i ^ 2) for i in range(count)])
        both = jnp.concatenate([value, across], axis=0)
        near = lax.ppermute(both, axis, [(i, i ^ 1) for i in range(count)])
        return jnp.concatenate([both, near], axis=0)
    return lax.all_gather(value, axis, axis=0, tiled=True)


def attention_kernel(piece_count, pairs, q_ref, *refs):
    key_refs = refs[:piece_count]
    value_refs = refs[piece_count : 2 * piece_count]
    bias_refs = refs[2 * piece_count : 3 * piece_count]
    rk_ref, rv_ref, w_ref, out_ref, mixed_ref = refs[3 * piece_count :]
    lane = lax.broadcasted_iota(jnp.int32, (1, LANES), 1)
    dims = (((1,), (1,)), ((), ()))
    rows = q_ref.shape[0]
    per_pair = LANES // HEAD_DIM
    for pair in range(pairs):
        cols = slice(pair * LANES, (pair + 1) * LANES)
        queries = q_ref[:, cols]
        stacked = jnp.concatenate(
            [jnp.where((lane // HEAD_DIM) == head, queries, jnp.zeros_like(queries)) for head in range(per_pair)],
            axis=0,
        )
        scores = [
            lax.dot_general(stacked, key_refs[p][:, cols], dims, preferred_element_type=jnp.float32) * SCALE
            + jnp.concatenate([bias_refs[p][...]] * per_pair, axis=0)
            for p in range(piece_count)
        ]
        peak = jnp.max(scores[0], axis=1, keepdims=True)
        for p in range(1, piece_count):
            peak = jnp.maximum(peak, jnp.max(scores[p], axis=1, keepdims=True))
        total = None
        summed = None
        for p in range(piece_count):
            weights = jnp.exp(scores[p] - peak)
            part_total = jnp.sum(weights, axis=1, keepdims=True)
            part = jnp.dot(weights.astype(jnp.bfloat16), value_refs[p][:, cols], preferred_element_type=jnp.float32)
            total = part_total if total is None else total + part_total
            summed = part if summed is None else summed + part
        view_part = summed / total
        ref_scores = lax.dot_general(stacked, rk_ref[:, cols], dims, preferred_element_type=jnp.float32) * SCALE
        ref_peak = jnp.max(ref_scores, axis=1, keepdims=True)
        ref_weights = jnp.exp(ref_scores - ref_peak)
        ref_total = jnp.sum(ref_weights, axis=1, keepdims=True)
        ref_summed = jnp.dot(ref_weights.astype(jnp.bfloat16), rv_ref[:, cols], preferred_element_type=jnp.float32)
        both = view_part + ref_summed / ref_total
        mixed = both[(per_pair - 1) * rows :]
        for head in range(per_pair - 1):
            mixed = jnp.where((lane // HEAD_DIM) == head, both[head * rows : (head + 1) * rows], mixed)
        mixed_ref[:, cols] = mixed.astype(mixed_ref.dtype)
    out_ref[...] = jnp.dot(mixed_ref[...], w_ref[...], preferred_element_type=jnp.float32).astype(out_ref.dtype)


def attention(queries, key_pieces, value_pieces, biases, ref_keys, ref_values, out_weight):
    rows, width = queries.shape
    span = width
    column = lambda j: (0, j)
    fixed = lambda j: (0, 0)
    in_specs = [pl.BlockSpec((rows, span), column)]
    in_specs += [pl.BlockSpec((piece.shape[0], span), column) for piece in key_pieces]
    in_specs += [pl.BlockSpec((piece.shape[0], span), column) for piece in value_pieces]
    in_specs += [pl.BlockSpec(bias.shape, fixed) for bias in biases]
    in_specs += [pl.BlockSpec((ref_keys.shape[0], span), column)] * 2
    in_specs.append(pl.BlockSpec(out_weight.shape, fixed))
    keys = sum(piece.shape[0] for piece in key_pieces) + ref_keys.shape[0]
    return pl.pallas_call(
        functools.partial(attention_kernel, len(key_pieces), span // LANES),
        grid=(1,),
        scratch_shapes=[pltpu.VMEM((rows, width), jnp.bfloat16)],
        in_specs=in_specs,
        out_specs=pl.BlockSpec((rows, span), column),
        out_shape=jax.ShapeDtypeStruct((rows, width), jnp.bfloat16),
        compiler_params=pltpu.CompilerParams(
            dimension_semantics=("arbitrary",), vmem_limit_bytes=60 * 1024 * 1024
        ),
        cost_estimate=pl.CostEstimate(
            flops=8 * rows * keys * width + 2 * rows * width * width,
            transcendentals=2 * rows * keys * HEADS,
            bytes_accessed=2 * (2 * rows + 2 * keys) * width + 4 * rows * keys,
        ),
    )(queries, *key_pieces, *value_pieces, *biases, ref_keys, ref_values, out_weight)


def key_bias(query_views, query_adjacent, position, rows, shard_rows, view_tok):
    key_rows = position * shard_rows + jnp.arange(rows, dtype=jnp.int32)
    key_views = key_rows // view_tok
    keep = query_views[:, None] == key_views[None, :]
    for slot in range(ADJ):
        keep = keep | (query_adjacent[:, slot : slot + 1] == key_views[None, :].astype(jnp.float32))
    return jnp.where(keep, 0.0, -jnp.inf).astype(jnp.float32)


def body(queries, keys, values, ref_keys, ref_values, out_weight, adjacency, ref_source):
    shard_rows, width = queries.shape
    view_count = lax.axis_size("view")
    view_index = lax.axis_index("view")
    view_tok = shard_rows * view_count // VIEWS

    ref_both = jnp.concatenate([ref_keys, ref_values], axis=1)
    ref_shared = tree_broadcast(ref_both, "mesh", ref_source[0])
    if view_count == 4:
        across = lax.ppermute((keys, values), "view", [(i, i ^ 2) for i in range(view_count)])
        near = lax.ppermute((keys, values), "view", [(i, i ^ 1) for i in range(view_count)])
        ref_shared, across = lax.optimization_barrier((ref_shared, across))
        far = lax.ppermute(across, "view", [(i, i ^ 1) for i in range(view_count)])
        pieces = [(keys, values), near, across, far]
        positions = [view_index, view_index ^ 1, view_index ^ 2, view_index ^ 3]
    else:
        pieces = [lax.all_gather((keys, values), "view", axis=0, tiled=True)]
        positions = [jnp.zeros((), jnp.int32)]
    ref_all = gather_rows(ref_shared, "view")

    view_ids = jnp.arange(VIEWS, dtype=jnp.int32)
    query_views = (view_index * shard_rows + jnp.arange(shard_rows, dtype=jnp.int32)) // view_tok
    query_onehot = (query_views[:, None] == view_ids[None, :]).astype(jnp.float32)
    query_adjacent = jnp.dot(query_onehot, adjacency.astype(jnp.float32))
    biases = [
        key_bias(query_views, query_adjacent, position, piece[0].shape[0], shard_rows, view_tok)
        for piece, position in zip(pieces, positions)
    ]

    mixed = attention(
        queries,
        [piece[0] for piece in pieces],
        [piece[1] for piece in pieces],
        biases,
        ref_all[:, :width],
        ref_all[:, width:],
        out_weight,
    )
    return mixed


def solution(mesh):
    return jax.shard_map(
        body,
        mesh=mesh,
        in_specs=(
            P(("mesh", "view"), None),
            P(("mesh", "view"), None),
            P(("mesh", "view"), None),
            P(("mesh", "view"), None),
            P(("mesh", "view"), None),
            P(),
            P("mesh", None),
            P(),
        ),
        out_specs=P(("mesh", "view"), None),
        check_vma=False,
    )
```

```python
import functools

import jax
import jax.numpy as jnp
from jax import lax
from jax.experimental import pallas as pl
from jax.experimental.pallas import tpu as pltpu
from jax.sharding import PartitionSpec as P

HEADS = 20
HEAD_DIM = 64
VIEWS = 6
ADJ = 3
SCALE = 0.125
LANES = 128


def tree_broadcast(value, axis, source):
    count = lax.axis_size(axis)
    index = lax.axis_index(axis)
    if count & (count - 1):
        kept = jnp.where(index == source, value, jnp.zeros_like(value))
        return lax.psum(kept, axis)
    distance = 1
    while distance < count:
        pairs = [(i, i ^ distance) for i in range(count)]
        received = lax.ppermute(value, axis, pairs)
        partner_has = ((index ^ distance) // distance) == (source // distance)
        value = jnp.where(partner_has, received, value)
        distance *= 2
    return value


def gather_rows(value, axis):
    count = lax.axis_size(axis)
    if count == 4:
        across = lax.ppermute(value, axis, [(i, i ^ 2) for i in range(count)])
        both = jnp.concatenate([value, across], axis=0)
        near = lax.ppermute(both, axis, [(i, i ^ 1) for i in range(count)])
        return jnp.concatenate([both, near], axis=0)
    return lax.all_gather(value, axis, axis=0, tiled=True)


def attention_kernel(piece_count, pairs, q_ref, *refs):
    key_refs = refs[:piece_count]
    value_refs = refs[piece_count : 2 * piece_count]
    bias_refs = refs[2 * piece_count : 3 * piece_count]
    rk_ref, rv_ref, out_ref = refs[3 * piece_count :]
    lane = lax.broadcasted_iota(jnp.int32, (1, LANES), 1)
    dims = (((1,), (1,)), ((), ()))
    rows = q_ref.shape[0]
    per_pair = LANES // HEAD_DIM
    for pair in range(pairs):
        cols = slice(pair * LANES, (pair + 1) * LANES)
        queries = q_ref[:, cols]
        stacked = jnp.concatenate(
            [jnp.where((lane // HEAD_DIM) == head, queries, jnp.zeros_like(queries)) for head in range(per_pair)],
            axis=0,
        )
        scores = [
            lax.dot_general(stacked, key_refs[p][:, cols], dims, preferred_element_type=jnp.float32) * SCALE
            + jnp.concatenate([bias_refs[p][...]] * per_pair, axis=0)
            for p in range(piece_count)
        ]
        peak = jnp.max(scores[0], axis=1, keepdims=True)
        for p in range(1, piece_count):
            peak = jnp.maximum(peak, jnp.max(scores[p], axis=1, keepdims=True))
        total = None
        summed = None
        for p in range(piece_count):
            weights = jnp.exp(scores[p] - peak)
            part_total = jnp.sum(weights, axis=1, keepdims=True)
            part = jnp.dot(weights.astype(jnp.bfloat16), value_refs[p][:, cols], preferred_element_type=jnp.float32)
            total = part_total if total is None else total + part_total
            summed = part if summed is None else summed + part
        view_part = summed / total
        ref_scores = lax.dot_general(stacked, rk_ref[:, cols], dims, preferred_element_type=jnp.float32) * SCALE
        ref_peak = jnp.max(ref_scores, axis=1, keepdims=True)
        ref_weights = jnp.exp(ref_scores - ref_peak)
        ref_total = jnp.sum(ref_weights, axis=1, keepdims=True)
        ref_summed = jnp.dot(ref_weights.astype(jnp.bfloat16), rv_ref[:, cols], preferred_element_type=jnp.float32)
        both = view_part + ref_summed / ref_total
        mixed = both[(per_pair - 1) * rows :]
        for head in range(per_pair - 1):
            mixed = jnp.where((lane // HEAD_DIM) == head, both[head * rows : (head + 1) * rows], mixed)
        out_ref[:, cols] = mixed.astype(out_ref.dtype)


def attention(queries, key_pieces, value_pieces, biases, ref_keys, ref_values, steps):
    rows, width = queries.shape
    span = width // steps
    column = lambda j: (0, j)
    fixed = lambda j: (0, 0)
    in_specs = [pl.BlockSpec((rows, span), column)]
    in_specs += [pl.BlockSpec((piece.shape[0], span), column) for piece in key_pieces]
    in_specs += [pl.BlockSpec((piece.shape[0], span), column) for piece in value_pieces]
    in_specs += [pl.BlockSpec(bias.shape, fixed) for bias in biases]
    in_specs += [pl.BlockSpec((ref_keys.shape[0], span), column)] * 2
    keys = sum(piece.shape[0] for piece in key_pieces) + ref_keys.shape[0]
    return pl.pallas_call(
        functools.partial(attention_kernel, len(key_pieces), span // LANES),
        grid=(steps,),
        in_specs=in_specs,
        out_specs=pl.BlockSpec((rows, span), column),
        out_shape=jax.ShapeDtypeStruct((rows, width), jnp.bfloat16),
        compiler_params=pltpu.CompilerParams(
            dimension_semantics=("arbitrary",), vmem_limit_bytes=48 * 1024 * 1024
        ),
        cost_estimate=pl.CostEstimate(
            flops=8 * rows * keys * width,
            transcendentals=2 * rows * keys * HEADS,
            bytes_accessed=2 * (2 * rows + 2 * keys) * width + 4 * rows * keys,
        ),
    )(queries, *key_pieces, *value_pieces, *biases, ref_keys, ref_values)


def key_bias(query_views, query_adjacent, position, rows, shard_rows, view_tok):
    key_rows = position * shard_rows + jnp.arange(rows, dtype=jnp.int32)
    key_views = key_rows // view_tok
    keep = query_views[:, None] == key_views[None, :]
    for slot in range(ADJ):
        keep = keep | (query_adjacent[:, slot : slot + 1] == key_views[None, :].astype(jnp.float32))
    return jnp.where(keep, 0.0, -jnp.inf).astype(jnp.float32)


def body(queries, keys, values, ref_keys, ref_values, out_weight, adjacency, ref_source):
    shard_rows, width = queries.shape
    view_count = lax.axis_size("view")
    view_index = lax.axis_index("view")
    view_tok = shard_rows * view_count // VIEWS

    ref_both = jnp.concatenate([ref_keys, ref_values], axis=1)
    ref_shared = tree_broadcast(ref_both, "mesh", ref_source[0])
    if view_count == 4:
        across = lax.ppermute((keys, values), "view", [(i, i ^ 2) for i in range(view_count)])
        near = lax.ppermute((keys, values), "view", [(i, i ^ 1) for i in range(view_count)])
        ref_shared, unused = lax.optimization_barrier((ref_shared, across))
        far = lax.ppermute(across, "view", [(i, i ^ 1) for i in range(view_count)])
        pieces = [(keys, values), near, across, far]
        positions = [view_index, view_index ^ 1, view_index ^ 2, view_index ^ 3]
    else:
        pieces = [lax.all_gather((keys, values), "view", axis=0, tiled=True)]
        positions = [jnp.zeros((), jnp.int32)]
    ref_all = gather_rows(ref_shared, "view")

    view_ids = jnp.arange(VIEWS, dtype=jnp.int32)
    query_views = (view_index * shard_rows + jnp.arange(shard_rows, dtype=jnp.int32)) // view_tok
    query_onehot = (query_views[:, None] == view_ids[None, :]).astype(jnp.float32)
    query_adjacent = jnp.dot(query_onehot, adjacency.astype(jnp.float32))
    biases = [
        key_bias(query_views, query_adjacent, position, piece[0].shape[0], shard_rows, view_tok)
        for piece, position in zip(pieces, positions)
    ]

    mixed = attention(
        queries,
        [piece[0] for piece in pieces],
        [piece[1] for piece in pieces],
        biases,
        ref_all[:, :width],
        ref_all[:, width:],
        1,
    )
    return jnp.dot(mixed, out_weight, preferred_element_type=jnp.float32).astype(jnp.bfloat16)


def solution(mesh):
    return jax.shard_map(
        body,
        mesh=mesh,
        in_specs=(
            P(("mesh", "view"), None),
            P(("mesh", "view"), None),
            P(("mesh", "view"), None),
            P(("mesh", "view"), None),
            P(("mesh", "view"), None),
            P(),
            P("mesh", None),
            P(),
        ),
        out_specs=P(("mesh", "view"), None),
        check_vma=False,
    )
```
